512 devices in a mesh: dp: 64 (over z, y_hi, core), mp: 8 (over x, y_lo).
Axes of the slice: x: 4, y: 8 (y_hi: 4, y_lo: 2; y = y_hi * 2 + y_lo), z: 8, core: 2. Of those that a mesh axis runs over, the one named last changes fastest.
Arguments:
- queries: bfloat16 [32768, 8192], P('dp', 'mp'), may hold values from -45 to 45
- key_rows: bfloat16 [32768, 1024], P('dp', 'mp'), may hold values from -4 to 4
- value_rows: bfloat16 [32768, 1024], P('dp', 'mp'), may hold values from -6 to 6
- landmark_index: int32 [512], P('dp'), may hold values from 0 to 32767, as said below
- radius_in: float32 [512], replicated, may hold values from 0.5 to 4
- radius_out: float32 [512], replicated, may hold values from 0.02 to 0.5
Outputs:
- cross_covariance: float32 [512, 512], P('mp', 'dp')
The draws below stay inside these ranges and needn't reach their ends.
Inputs may be any that keep to these rules, and one draw needn't show every extreme that they name: `landmark_index`: the 8 landmarks held by index d of dp name distinct tokens of sequence d, that is, positions d * 512 to (d + 1) * 512 - 1.
All inputs are finite; a program needn't handle non-finite values.
Results may differ from the reference program's by a relative error of at most 0.003.
Values may be sent and summed in bfloat16 or wider, within the bound.
No kernel may reach another device: no remote copies, remote signals or barrier semaphores. Data moves between devices by JAX's collectives and lax.ppermute only.
A program may use at most 64 MiB of HBM per device.

```python
import math
import jax
import jax.numpy as jnp
from jax import lax

D = 8192
HEADS = 64
KV_HEADS = 8
HEAD_DIM = 128
SEQ = 512
LAND_DEV = 8
TOKENS = 32768
LANDMARKS = 512


def shared_keys(key):
    noise_key = jax.random.fold_in(key, 11)
    drawn = jnp.clip(jax.random.normal(noise_key, (TOKENS, KV_HEADS * HEAD_DIM), jnp.float32), -4.0, 4.0)
    return drawn


def draw_key_rows(key, part):
    return shared_keys(key).astype(jnp.bfloat16)


def draw_queries(key, part):
    noise_key, scale_key = jax.random.split(jax.random.fold_in(key, 23))
    common_key, factor_key = jax.random.split(jax.random.fold_in(key, 29))
    sequences = TOKENS // SEQ
    position = jnp.arange(TOKENS, dtype=jnp.float32) / TOKENS
    within = (jnp.arange(TOKENS, dtype=jnp.int32) % SEQ).astype(jnp.float32) / SEQ
    noise = jnp.clip(jax.random.normal(noise_key, (TOKENS, D), jnp.float32), -5.0, 5.0)
    common = jnp.clip(jax.random.normal(common_key, (sequences, D), jnp.float32), -4.0, 4.0)
    spread = jnp.exp(jax.random.uniform(scale_key, (TOKENS, 1), jnp.float32, -0.25, 0.25))
    factor = jnp.exp(jax.random.uniform(factor_key, (sequences,), jnp.float32, -0.5, 0.5))
    mixed = 0.6 * noise.reshape(sequences, SEQ, D) + 0.8 * common[:, None, :]
    mixed = mixed * factor[:, None, None]
    trend = (0.6 + 0.6 * position) * (0.7 + 0.6 * within)
    drawn = mixed.reshape(TOKENS, D) * spread * trend[:, None]
    return drawn.astype(jnp.bfloat16)


def draw_landmark_index(key, part):
    sequences = TOKENS // SEQ
    block_keys = jax.random.split(jax.random.fold_in(key, 31), sequences)

    def pick_block(block_key):
        return jax.random.permutation(block_key, SEQ // 4)[:LAND_DEV].astype(jnp.int32)
    chosen = jax.vmap(pick_block)(block_keys)
    block_index = jnp.arange(sequences, dtype=jnp.int32)
    offset = jnp.where(block_index == 0, -chosen[:, 0], jnp.where(block_index == sequences - 1, SEQ - 1 - chosen[:, 0], 0))
    chosen = (chosen + offset[:, None]) % SEQ
    return (chosen + block_index[:, None] * SEQ).reshape(sequences * LAND_DEV).astype(jnp.int32)


def level_of(stream_key, shape, cuts, least, top_value):
    loudness = 1.0
    for dim, blocks in cuts:
        heights = jax.random.uniform(jax.random.fold_in(jax.random.fold_in(stream_key, 6), dim), (blocks,), jnp.float32, least / len(cuts), top_value / len(cuts))
        loudness = loudness * jnp.repeat(jnp.exp(heights), shape[dim] // blocks).reshape((-1,) + (1,) * (len(shape) - 1 - dim))
    return loudness


def scatter_about(stream_key, extent, deviation, limit, pieces=(), kind=jnp.bfloat16):
    values = deviation * jax.random.normal(stream_key, extent, jnp.float32)
    if pieces:
        values = values * level_of(stream_key, extent, pieces, -0.22, 0.18)
    return jnp.clip(values, -limit, limit).astype(kind)


def setup_inputs(seed: int = 0) -> dict:
    splits = jax.random.split(jax.random.key(seed), 7)
    return {
        "queries": draw_queries(jax.random.fold_in(splits[6], 71), 0),
        "key_rows": draw_key_rows(jax.random.fold_in(splits[6], 71), 0),
        "value_rows": scatter_about(splits[2], (TOKENS, KV_HEADS * HEAD_DIM), 1.0, 6.0, ((0, 64), (1, 8))),
        "landmark_index": draw_landmark_index(jax.random.fold_in(splits[6], 71), 0),
        "radius_in": jnp.clip(jnp.exp(jax.random.uniform(splits[4], (LANDMARKS,), jnp.float32, math.log(0.5), math.log(4.0))), 0.5, 4.0),
        "radius_out": jnp.clip(jnp.exp(jax.random.uniform(splits[5], (LANDMARKS,), jnp.float32, math.log(0.02), math.log(0.5))), 0.02, 0.5),
    }


EPSILON = 1e-06

def attend_sequence(blocks):
    query_block, key_block, value_block = blocks
    group_size = HEADS // KV_HEADS
    query_four = query_block.reshape(SEQ, KV_HEADS, group_size, HEAD_DIM).astype(jnp.float32)
    key_three = key_block.reshape(SEQ, KV_HEADS, HEAD_DIM).astype(jnp.float32)
    value_three = value_block.reshape(SEQ, KV_HEADS, HEAD_DIM).astype(jnp.float32)
    scores = jnp.einsum('tkgd,skd->kgts', query_four, key_three, precision=lax.Precision.HIGHEST) / math.sqrt(HEAD_DIM)
    row_position = lax.broadcasted_iota(jnp.int32, (SEQ, SEQ), 0)
    column_position = lax.broadcasted_iota(jnp.int32, (SEQ, SEQ), 1)
    scores = jnp.where(column_position <= row_position, scores, -jnp.inf)
    weights = jax.nn.softmax(scores, axis=-1).astype(jnp.bfloat16)
    mixture = jnp.einsum('kgts,skd->tkgd', weights.astype(jnp.float32), value_three, precision=lax.Precision.HIGHEST)
    return mixture.astype(jnp.bfloat16).reshape(SEQ, HEADS * HEAD_DIM)

def kernel_features(rows_block, landmark_rows, widths):
    row_norms = lax.optimization_barrier(jnp.sum(jnp.square(rows_block.astype(jnp.float32)), axis=1))
    mark_norms = lax.optimization_barrier(jnp.sum(jnp.square(landmark_rows.astype(jnp.float32)), axis=1))
    cross = jnp.dot(rows_block, landmark_rows.T, preferred_element_type=jnp.float32)
    distance = row_norms[:, None] + mark_norms[None, :] - 2.0 * cross
    return jnp.exp(-distance / (D * widths[None, :])).astype(jnp.bfloat16)

def reference(queries, key_rows, value_rows, landmark_index, radius_in, radius_out):
    sequences = TOKENS // SEQ
    attended = lax.map(attend_sequence, (queries.reshape(sequences, SEQ, D), key_rows.reshape(sequences, SEQ, KV_HEADS * HEAD_DIM), value_rows.reshape(sequences, SEQ, KV_HEADS * HEAD_DIM)))
    attended = attended.reshape(TOKENS, D)
    in_marks = jnp.take(queries, landmark_index, axis=0)
    out_marks = jnp.take(attended, landmark_index, axis=0)

    def feature_pair(blocks):
        query_block, attended_block = blocks
        return (kernel_features(query_block, in_marks, radius_in), kernel_features(attended_block, out_marks, radius_out))
    features_in, features_out = lax.map(feature_pair, (queries.reshape(sequences, SEQ, D), attended.reshape(sequences, SEQ, D)))
    features_in = features_in.reshape(TOKENS, LANDMARKS)
    features_out = features_out.reshape(TOKENS, LANDMARKS)
    mean_in = lax.optimization_barrier(jnp.sum(features_in.astype(jnp.float32), axis=0)) / TOKENS
    mean_out = lax.optimization_barrier(jnp.sum(features_out.astype(jnp.float32), axis=0)) / TOKENS
    centered_in = (features_in.astype(jnp.float32) - mean_in[None, :]).astype(jnp.bfloat16)
    centered_out = (features_out.astype(jnp.float32) - mean_out[None, :]).astype(jnp.bfloat16)
    spread_in = lax.optimization_barrier(jnp.sum(jnp.square(centered_in.astype(jnp.float32)), axis=0)) / TOKENS
    spread_out = lax.optimization_barrier(jnp.sum(jnp.square(centered_out.astype(jnp.float32)), axis=0)) / TOKENS
    covariance = jnp.dot(centered_in.T, centered_out, preferred_element_type=jnp.float32) / TOKENS
    return covariance / jnp.sqrt((spread_in + EPSILON)[:, None] * (spread_out + EPSILON)[None, :])
```

```python
import math

import jax
import jax.numpy as jnp
from jax import lax
from jax.sharding import PartitionSpec as P

D = 8192
HEAD_DIM = 128


EPSILON = 1e-06


def attend(queries, key_rows, value_rows):
    length = queries.shape[0]
    kv_heads = key_rows.shape[1] // HEAD_DIM
    group_size = queries.shape[1] // HEAD_DIM // kv_heads
    query_four = queries.reshape(length, kv_heads, group_size, HEAD_DIM)
    key_three = key_rows.reshape(length, kv_heads, HEAD_DIM)
    value_three = value_rows.reshape(length, kv_heads, HEAD_DIM)
    scores = jnp.einsum(
        "tkgd,skd->kgts", query_four, key_three, preferred_element_type=jnp.float32
    ) / math.sqrt(HEAD_DIM)
    row_position = lax.broadcasted_iota(jnp.int32, (length, length), 0)
    column_position = lax.broadcasted_iota(jnp.int32, (length, length), 1)
    scores = jnp.where(column_position <= row_position, scores, -jnp.inf)
    weights = jax.nn.softmax(scores, axis=-1).astype(jnp.bfloat16)
    mixture = jnp.einsum(
        "kgts,skd->tkgd", weights, value_three, preferred_element_type=jnp.float32
    )
    return mixture.astype(jnp.bfloat16).reshape(length, queries.shape[1])


def squares_by_row(matrix):
    return jnp.sum(jnp.square(matrix.astype(jnp.float32)), axis=-1)


def inner_rows(left, right):
    return lax.dot_general(
        left, right, (((1,), (1,)), ((), ())), preferred_element_type=jnp.float32
    )


def broadcast_gather(piece, axis_name):
    count = lax.axis_size(axis_name)
    spread = jnp.broadcast_to(piece[None], (count,) + piece.shape)
    return lax.all_to_all(spread, axis_name, 0, 0, tiled=True)


def shards(queries, key_rows, value_rows, landmark_index, radius_in, radius_out):
    length = queries.shape[0]
    model_count = lax.axis_size("mp")
    data_count = lax.axis_size("dp")
    model_index = lax.axis_index("mp")
    landmarks = radius_in.shape[0]
    row_share = landmarks // model_count
    column_share = landmarks // data_count
    token_count = length * data_count

    attended = attend(queries, key_rows, value_rows)

    own_rows = landmark_index % length
    landmark_rows = jnp.stack(
        [jnp.take(queries, own_rows, axis=0), jnp.take(attended, own_rows, axis=0)]
    )
    gathered = broadcast_gather(landmark_rows, "dp")
    landmark_piece = jnp.transpose(gathered, (1, 0, 2, 3)).reshape(
        2, landmarks, queries.shape[1]
    )

    row_norms = jnp.stack([squares_by_row(queries), squares_by_row(attended)])
    mark_norms = squares_by_row(landmark_piece)
    cross = jnp.stack(
        [inner_rows(queries, landmark_piece[0]), inner_rows(attended, landmark_piece[1])]
    )
    distance_part = row_norms[:, :, None] + mark_norms[:, None, :] - 2.0 * cross
    distance_part = distance_part.reshape(2, length, model_count, row_share)
    distance = jnp.sum(
        lax.all_to_all(distance_part, "mp", 2, 2, tiled=True), axis=2
    )

    widths = lax.dynamic_slice_in_dim(
        jnp.stack([radius_in, radius_out]), model_index * row_share, row_share, 1
    )
    features = jnp.exp(-distance / (D * widths[:, None, :])).astype(jnp.bfloat16)
    row_features = features[0]
    column_features = jnp.transpose(
        broadcast_gather(features[1], "mp"), (1, 0, 2)
    ).reshape(length, landmarks)

    rows32 = row_features.astype(jnp.float32)
    columns32 = column_features.astype(jnp.float32)
    row_mean = jnp.mean(rows32, axis=0)
    column_mean = jnp.mean(columns32, axis=0)
    rows_centered = rows32 - row_mean[None, :]
    columns_centered = columns32 - column_mean[None, :]
    second = lax.dot_general(
        rows_centered,
        columns_centered,
        (((0,), (0,)), ((), ())),
        precision=lax.Precision.HIGHEST,
        preferred_element_type=jnp.float32,
    )
    row_square = jnp.sum(jnp.square(rows_centered), axis=0)
    column_square = jnp.sum(jnp.square(columns_centered), axis=0)

    packed = jnp.concatenate(
        [
            jnp.transpose(
                second.reshape(row_share, data_count, column_share), (1, 0, 2)
            ).reshape(data_count, row_share * column_share),
            jnp.broadcast_to(row_mean[None], (data_count, row_share)),
            jnp.broadcast_to(row_square[None], (data_count, row_share)),
            column_mean.reshape(data_count, column_share),
            column_square.reshape(data_count, column_share),
        ],
        axis=1,
    )
    received = lax.all_to_all(packed, "dp", 0, 0, tiled=True)
    cut = row_share * column_share
    second_parts = received[:, :cut].reshape(data_count, row_share, column_share)
    row_means = received[:, cut : cut + row_share]
    row_squares = received[:, cut + row_share : cut + 2 * row_share]
    column_means = received[:, cut + 2 * row_share : cut + 2 * row_share + column_share]
    column_squares = received[:, cut + 2 * row_share + column_share :]

    row_shift = row_means - jnp.mean(row_means, axis=0)[None, :]
    column_shift = column_means - jnp.mean(column_means, axis=0)[None, :]
    between = jnp.sum(row_shift[:, :, None] * column_shift[:, None, :], axis=0)
    covariance = (jnp.sum(second_parts, axis=0) + length * between) / token_count
    spread_rows = (
        jnp.sum(row_squares, axis=0) + length * jnp.sum(jnp.square(row_shift), axis=0)
    ) / token_count
    spread_columns = (
        jnp.sum(column_squares, axis=0)
        + length * jnp.sum(jnp.square(column_shift), axis=0)
    ) / token_count
    return covariance / jnp.sqrt(
        (spread_rows + EPSILON)[:, None] * (spread_columns + EPSILON)[None, :]
    )


def solution(mesh):
    return jax.shard_map(
        shards,
        mesh=mesh,
        in_specs=(P("dp", "mp"), P("dp", "mp"), P("dp", "mp"), P("dp"), P(), P()),
        out_specs=P("mp", "dp"),
        check_vma=False,
    )
```

```python
import math

import jax
import jax.numpy as jnp
from jax import lax
from jax.sharding import Mesh, PartitionSpec as P

D = 8192
HEAD_DIM = 128


EPSILON = 1e-06

CHIPS = ("z", "y_hi")
CORE = "core"
DATA = CHIPS + (CORE,)
MODEL = ("x", "y_lo")


def attend(queries, key_rows, value_rows):
    length = queries.shape[0]
    kv_heads = key_rows.shape[1] // HEAD_DIM
    group_size = queries.shape[1] // HEAD_DIM // kv_heads
    query_four = queries.reshape(length, kv_heads, group_size, HEAD_DIM)
    key_three = key_rows.reshape(length, kv_heads, HEAD_DIM)
    value_three = value_rows.reshape(length, kv_heads, HEAD_DIM)
    scores = jnp.einsum(
        "tkgd,skd->kgts", query_four, key_three, preferred_element_type=jnp.float32
    ) / math.sqrt(HEAD_DIM)
    row_position = lax.broadcasted_iota(jnp.int32, (length, length), 0)
    column_position = lax.broadcasted_iota(jnp.int32, (length, length), 1)
    scores = jnp.where(column_position <= row_position, scores, -jnp.inf)
    weights = jax.nn.softmax(scores, axis=-1).astype(jnp.bfloat16)
    mixture = jnp.einsum(
        "kgts,skd->tkgd", weights, value_three, preferred_element_type=jnp.float32
    )
    return mixture.astype(jnp.bfloat16).reshape(length, queries.shape[1])


def squares_by_row(matrix):
    return jnp.sum(jnp.square(matrix.astype(jnp.float32)), axis=-1)


def inner_rows(left, right):
    return lax.dot_general(
        left, right, (((1,), (1,)), ((), ())), preferred_element_type=jnp.float32
    )


def attend_rows(queries, key_rows, value_rows, rows):
    length = queries.shape[0]
    kv_heads = key_rows.shape[1] // HEAD_DIM
    group_size = queries.shape[1] // HEAD_DIM // kv_heads
    picked = jnp.take(queries, rows, axis=0)
    query_four = picked.reshape(rows.shape[0], kv_heads, group_size, HEAD_DIM)
    key_three = key_rows.reshape(length, kv_heads, HEAD_DIM)
    value_three = value_rows.reshape(length, kv_heads, HEAD_DIM)
    scores = jnp.einsum(
        "tkgd,skd->kgts", query_four, key_three, preferred_element_type=jnp.float32
    ) / math.sqrt(HEAD_DIM)
    column_position = lax.broadcasted_iota(jnp.int32, (rows.shape[0], length), 1)
    scores = jnp.where(column_position <= rows[:, None], scores, -jnp.inf)
    weights = jax.nn.softmax(scores, axis=-1).astype(jnp.bfloat16)
    mixture = jnp.einsum(
        "kgts,skd->tkgd", weights, value_three, preferred_element_type=jnp.float32
    )
    return mixture.astype(jnp.bfloat16).reshape(rows.shape[0], queries.shape[1])


def swap_cores(piece):
    return lax.ppermute(piece, CORE, [(0, 1), (1, 0)])


def gather_marks(query_marks, output_marks):
    core = lax.axis_index(CORE)
    own = jnp.stack([query_marks, output_marks])
    other = swap_cores(own)
    first = core == 0
    pair = jnp.where(first, jnp.stack([own, other], 1), jnp.stack([other, own], 1))
    mine = jnp.where(first, pair[0], pair[1])
    fetched = broadcast_gather(mine, CHIPS)
    swapped = swap_cores(fetched)
    query_rows = jnp.where(first, fetched, swapped)
    output_rows = jnp.where(first, swapped, fetched)
    return jnp.stack([query_rows, output_rows])


def broadcast_gather(piece, axis_name):
    count = lax.axis_size(axis_name)
    spread = jnp.broadcast_to(piece[None], (count,) + piece.shape)
    return lax.all_to_all(spread, axis_name, 0, 0, tiled=True)


def shards(queries, key_rows, value_rows, landmark_index, radius_in, radius_out):
    length = queries.shape[0]
    model_count = lax.axis_size(MODEL)
    data_count = lax.axis_size(DATA)
    model_index = lax.axis_index(MODEL)
    landmarks = radius_in.shape[0]
    row_share = landmarks // model_count
    column_share = landmarks // data_count
    token_count = length * data_count

    own_rows = landmark_index % length
    gathered = gather_marks(
        jnp.take(queries, own_rows, axis=0),
        attend_rows(queries, key_rows, value_rows, own_rows),
    )
    landmark_piece = gathered.reshape(2, landmarks, queries.shape[1])
    attended = attend(queries, key_rows, value_rows)

    row_norms = jnp.stack([squares_by_row(queries), squares_by_row(attended)])
    mark_norms = squares_by_row(landmark_piece)
    cross = jnp.stack(
        [inner_rows(queries, landmark_piece[0]), inner_rows(attended, landmark_piece[1])]
    )
    distance_part = row_norms[:, :, None] + mark_norms[:, None, :] - 2.0 * cross
    distance_part = distance_part.reshape(2, length, model_count, row_share)
    distance = jnp.sum(
        lax.all_to_all(distance_part, MODEL, 2, 2, tiled=True), axis=2
    )

    widths = lax.dynamic_slice_in_dim(
        jnp.stack([radius_in, radius_out]), model_index * row_share, row_share, 1
    )
    features = jnp.exp(-distance / (D * widths[:, None, :])).astype(jnp.bfloat16)
    row_features = features[0]
    column_features = jnp.transpose(
        broadcast_gather(features[1], MODEL), (1, 0, 2)
    ).reshape(length, landmarks)

    rows32 = row_features.astype(jnp.float32)
    columns32 = column_features.astype(jnp.float32)
    row_mean = jnp.mean(rows32, axis=0)
    column_mean = jnp.mean(columns32, axis=0)
    rows_centered = rows32 - row_mean[None, :]
    columns_centered = columns32 - column_mean[None, :]
    second = lax.dot_general(
        rows_centered,
        columns_centered,
        (((0,), (0,)), ((), ())),
        precision=lax.Precision.HIGHEST,
        preferred_element_type=jnp.float32,
    )
    row_square = jnp.sum(jnp.square(rows_centered), axis=0)
    column_square = jnp.sum(jnp.square(columns_centered), axis=0)

    packed = jnp.concatenate(
        [
            jnp.transpose(
                second.reshape(row_share, data_count, column_share), (1, 0, 2)
            ).reshape(data_count, row_share * column_share),
            jnp.broadcast_to(row_mean[None], (data_count, row_share)),
            jnp.broadcast_to(row_square[None], (data_count, row_share)),
            column_mean.reshape(data_count, column_share),
            column_square.reshape(data_count, column_share),
        ],
        axis=1,
    )
    received = lax.all_to_all(packed, DATA, 0, 0, tiled=True)
    cut = row_share * column_share
    second_parts = received[:, :cut].reshape(data_count, row_share, column_share)
    row_means = received[:, cut : cut + row_share]
    row_squares = received[:, cut + row_share : cut + 2 * row_share]
    column_means = received[:, cut + 2 * row_share : cut + 2 * row_share + column_share]
    column_squares = received[:, cut + 2 * row_share + column_share :]

    row_shift = row_means - jnp.mean(row_means, axis=0)[None, :]
    column_shift = column_means - jnp.mean(column_means, axis=0)[None, :]
    between = jnp.sum(row_shift[:, :, None] * column_shift[:, None, :], axis=0)
    covariance = (jnp.sum(second_parts, axis=0) + length * between) / token_count
    spread_rows = (
        jnp.sum(row_squares, axis=0) + length * jnp.sum(jnp.square(row_shift), axis=0)
    ) / token_count
    spread_columns = (
        jnp.sum(column_squares, axis=0)
        + length * jnp.sum(jnp.square(column_shift), axis=0)
    ) / token_count
    return covariance / jnp.sqrt(
        (spread_rows + EPSILON)[:, None] * (spread_columns + EPSILON)[None, :]
    )


def solution(mesh):
    data_count, model_count = mesh.devices.shape
    chips = mesh.devices.reshape(data_count // 8, 4, 2, model_count // 2, 2)
    split = Mesh(chips, DATA + MODEL)
    return jax.shard_map(
        shards,
        mesh=split,
        in_specs=(P(DATA, MODEL), P(DATA, MODEL), P(DATA, MODEL), P(DATA), P(), P()),
        out_specs=P(MODEL, DATA),
        check_vma=False,
    )
```

```python
import math

import jax
import jax.numpy as jnp
from jax import lax
from jax.sharding import Mesh, PartitionSpec as P

D = 8192
HEAD_DIM = 128


EPSILON = 1e-06

CHIPS = ("z", "y_hi")
CORE = "core"
DATA = CHIPS + (CORE,)
MODEL = ("x", "y_lo")


def attend(queries, key_rows, value_rows):
    length = queries.shape[0]
    kv_heads = key_rows.shape[1] // HEAD_DIM
    group_size = queries.shape[1] // HEAD_DIM // kv_heads
    query_four = queries.reshape(length, kv_heads, group_size, HEAD_DIM)
    key_three = key_rows.reshape(length, kv_heads, HEAD_DIM)
    value_three = value_rows.reshape(length, kv_heads, HEAD_DIM)
    scores = jnp.einsum(
        "tkgd,skd->kgts", query_four, key_three, preferred_element_type=jnp.float32
    ) / math.sqrt(HEAD_DIM)
    row_position = lax.broadcasted_iota(jnp.int32, (length, length), 0)
    column_position = lax.broadcasted_iota(jnp.int32, (length, length), 1)
    scores = jnp.where(column_position <= row_position, scores, -jnp.inf)
    weights = jax.nn.softmax(scores, axis=-1).astype(jnp.bfloat16)
    mixture = jnp.einsum(
        "kgts,skd->tkgd", weights, value_three, preferred_element_type=jnp.float32
    )
    return mixture.astype(jnp.bfloat16).reshape(length, queries.shape[1])


def squares_by_row(matrix):
    return jnp.sum(jnp.square(matrix.astype(jnp.float32)), axis=-1)


def inner_rows(left, right):
    return lax.dot_general(
        left, right, (((1,), (1,)), ((), ())), preferred_element_type=jnp.float32
    )


def attend_rows(queries, key_rows, value_rows, rows):
    length = queries.shape[0]
    kv_heads = key_rows.shape[1] // HEAD_DIM
    group_size = queries.shape[1] // HEAD_DIM // kv_heads
    picked = jnp.take(queries, rows, axis=0)
    query_four = picked.reshape(rows.shape[0], kv_heads, group_size, HEAD_DIM)
    key_three = key_rows.reshape(length, kv_heads, HEAD_DIM)
    value_three = value_rows.reshape(length, kv_heads, HEAD_DIM)
    scores = jnp.einsum(
        "tkgd,skd->kgts", query_four, key_three, preferred_element_type=jnp.float32
    ) / math.sqrt(HEAD_DIM)
    column_position = lax.broadcasted_iota(jnp.int32, (rows.shape[0], length), 1)
    scores = jnp.where(column_position <= rows[:, None], scores, -jnp.inf)
    weights = jax.nn.softmax(scores, axis=-1).astype(jnp.bfloat16)
    mixture = jnp.einsum(
        "kgts,skd->tkgd", weights, value_three, preferred_element_type=jnp.float32
    )
    return mixture.astype(jnp.bfloat16).reshape(rows.shape[0], queries.shape[1])


def swap_cores(piece):
    return lax.ppermute(piece, CORE, [(0, 1), (1, 0)])


def by_core(first, own_core, other_core, axis):
    return jnp.where(
        first,
        jnp.stack([own_core, other_core], axis),
        jnp.stack([other_core, own_core], axis),
    )


def merge_pair(count, second, row_mean, row_square, column_mean, column_square):
    pieces = (second, row_mean, row_square, column_mean, column_square)
    flat = swap_cores(jnp.concatenate([piece.reshape(-1) for piece in pieces]))
    other, start = [], 0
    for piece in pieces:
        other.append(flat[start : start + piece.size].reshape(piece.shape))
        start += piece.size
    row_gap = row_mean - other[1]
    column_gap = column_mean - other[3]
    half = 0.5 * count
    return (
        second + other[0] + half * row_gap[:, None] * column_gap[None, :],
        0.5 * (row_mean + other[1]),
        row_square + other[2] + half * jnp.square(row_gap),
        0.5 * (column_mean + other[3]),
        column_square + other[4] + half * jnp.square(column_gap),
    )


def broadcast_gather(piece, axis_name):
    count = lax.axis_size(axis_name)
    spread = jnp.broadcast_to(piece[None], (count,) + piece.shape)
    return lax.all_to_all(spread, axis_name, 0, 0, tiled=True)


def shards(queries, key_rows, value_rows, landmark_index, radius_in, radius_out):
    length = queries.shape[0]
    model_count = lax.axis_size(MODEL)
    data_count = lax.axis_size(DATA)
    model_index = lax.axis_index(MODEL)
    landmarks = radius_in.shape[0]
    row_share = landmarks // model_count
    column_share = landmarks // data_count
    token_count = length * data_count

    first = lax.axis_index(CORE) == 0
    own_rows = landmark_index % length
    marks = jnp.stack(
        [
            jnp.take(queries, own_rows, axis=0),
            attend_rows(queries, key_rows, value_rows, own_rows),
        ],
        1,
    )
    fetched = broadcast_gather(marks, CHIPS)
    swapped = swap_cores(fetched)
    attended = attend(queries, key_rows, value_rows)
    rows = jnp.stack([queries, attended])
    row_norms = squares_by_row(rows)

    def part_of(piece):
        marks_of = [piece[:, :, kind].reshape(-1, queries.shape[1]) for kind in range(2)]
        return jnp.stack(
            [
                squares_by_row(marks_of[kind])[None, :]
                - 2.0 * inner_rows(rows[kind], marks_of[kind])
                for kind in range(2)
            ]
        ).reshape(2, length, -1, marks.shape[0])

    distance_part = row_norms[:, :, None, None, None] + by_core(
        first, part_of(fetched), part_of(swapped), 3
    )
    distance_part = distance_part.reshape(2, length, model_count, row_share)
    distance = jnp.sum(
        lax.all_to_all(distance_part, MODEL, 2, 2, tiled=True), axis=2
    )

    widths = lax.dynamic_slice_in_dim(
        jnp.stack([radius_in, radius_out]), model_index * row_share, row_share, 1
    )
    features = jnp.exp(-distance / (D * widths[:, None, :])).astype(jnp.bfloat16)
    row_features = features[0]
    column_features = jnp.transpose(
        broadcast_gather(features[1], MODEL), (1, 0, 2)
    ).reshape(length, landmarks)

    rows32 = row_features.astype(jnp.float32)
    columns32 = column_features.astype(jnp.float32)
    row_mean = jnp.mean(rows32, axis=0)
    column_mean = jnp.mean(columns32, axis=0)
    rows_centered = rows32 - row_mean[None, :]
    columns_centered = columns32 - column_mean[None, :]
    second = lax.dot_general(
        rows_centered,
        columns_centered,
        (((0,), (0,)), ((), ())),
        precision=lax.Precision.HIGHEST,
        preferred_element_type=jnp.float32,
    )
    row_square = jnp.sum(jnp.square(rows_centered), axis=0)
    column_square = jnp.sum(jnp.square(columns_centered), axis=0)

    second, row_mean, row_square, column_mean, column_square = merge_pair(
        length, second, row_mean, row_square, column_mean, column_square
    )
    chip_count = data_count // 2

    def for_core(values):
        split = values.reshape(values.shape[:-1] + (chip_count, 2, column_share))
        return jnp.where(first, split[..., 0, :], split[..., 1, :])

    packed = jnp.concatenate(
        [
            jnp.transpose(for_core(second), (1, 0, 2)).reshape(
                chip_count, row_share * column_share
            ),
            jnp.broadcast_to(row_mean[None], (chip_count, row_share)),
            jnp.broadcast_to(row_square[None], (chip_count, row_share)),
            for_core(column_mean),
            for_core(column_square),
        ],
        axis=1,
    )
    received = lax.all_to_all(packed, CHIPS, 0, 0, tiled=True)
    cut = row_share * column_share
    second_parts = received[:, :cut].reshape(chip_count, row_share, column_share)
    row_means = received[:, cut : cut + row_share]
    row_squares = received[:, cut + row_share : cut + 2 * row_share]
    column_means = received[:, cut + 2 * row_share : cut + 2 * row_share + column_share]
    column_squares = received[:, cut + 2 * row_share + column_share :]
    length = 2 * length

    row_shift = row_means - jnp.mean(row_means, axis=0)[None, :]
    column_shift = column_means - jnp.mean(column_means, axis=0)[None, :]
    between = jnp.sum(row_shift[:, :, None] * column_shift[:, None, :], axis=0)
    covariance = (jnp.sum(second_parts, axis=0) + length * between) / token_count
    spread_rows = (
        jnp.sum(row_squares, axis=0) + length * jnp.sum(jnp.square(row_shift), axis=0)
    ) / token_count
    spread_columns = (
        jnp.sum(column_squares, axis=0)
        + length * jnp.sum(jnp.square(column_shift), axis=0)
    ) / token_count
    return covariance / jnp.sqrt(
        (spread_rows + EPSILON)[:, None] * (spread_columns + EPSILON)[None, :]
    )


def solution(mesh):
    data_count, model_count = mesh.devices.shape
    chips = mesh.devices.reshape(data_count // 8, 4, 2, model_count // 2, 2)
    split = Mesh(chips, DATA + MODEL)
    return jax.shard_map(
        shards,
        mesh=split,
        in_specs=(P(DATA, MODEL), P(DATA, MODEL), P(DATA, MODEL), P(DATA), P(), P()),
        out_specs=P(MODEL, DATA),
        check_vma=False,
    )
```

```python
import math

import jax
import jax.numpy as jnp
from jax import lax
from jax.sharding import Mesh, PartitionSpec as P

D = 8192
HEAD_DIM = 128


EPSILON = 1e-06

CHIPS = ("z", "y_hi")
CORE = "core"
DATA = CHIPS + (CORE,)
MODEL = ("x", "y_lo")


def attend(queries, key_rows, value_rows):
    length = queries.shape[0]
    kv_heads = key_rows.shape[1] // HEAD_DIM
    group_size = queries.shape[1] // HEAD_DIM // kv_heads
    query_four = queries.reshape(length, kv_heads, group_size, HEAD_DIM)
    key_three = key_rows.reshape(length, kv_heads, HEAD_DIM)
    value_three = value_rows.reshape(length, kv_heads, HEAD_DIM)
    scores = jnp.einsum(
        "tkgd,skd->kgts", query_four, key_three, preferred_element_type=jnp.float32
    ) / math.sqrt(HEAD_DIM)
    row_position = lax.broadcasted_iota(jnp.int32, (length, length), 0)
    column_position = lax.broadcasted_iota(jnp.int32, (length, length), 1)
    scores = jnp.where(column_position <= row_position, scores, -jnp.inf)
    weights = jax.nn.softmax(scores, axis=-1).astype(jnp.bfloat16)
    mixture = jnp.einsum(
        "kgts,skd->tkgd", weights, value_three, preferred_element_type=jnp.float32
    )
    return mixture.astype(jnp.bfloat16).reshape(length, queries.shape[1])


def squares_by_row(matrix):
    return jnp.sum(jnp.square(matrix.astype(jnp.float32)), axis=-1)


def inner_rows(left, right):
    return lax.dot_general(
        left, right, (((1,), (1,)), ((), ())), preferred_element_type=jnp.float32
    )


def attend_rows(queries, key_rows, value_rows, rows):
    length = queries.shape[0]
    kv_heads = key_rows.shape[1] // HEAD_DIM
    group_size = queries.shape[1] // HEAD_DIM // kv_heads
    picked = jnp.take(queries, rows, axis=0)
    query_four = picked.reshape(rows.shape[0], kv_heads, group_size, HEAD_DIM)
    key_three = key_rows.reshape(length, kv_heads, HEAD_DIM)
    value_three = value_rows.reshape(length, kv_heads, HEAD_DIM)
    scores = jnp.einsum(
        "tkgd,skd->kgts", query_four, key_three, preferred_element_type=jnp.float32
    ) / math.sqrt(HEAD_DIM)
    column_position = lax.broadcasted_iota(jnp.int32, (rows.shape[0], length), 1)
    scores = jnp.where(column_position <= rows[:, None], scores, -jnp.inf)
    weights = jax.nn.softmax(scores, axis=-1).astype(jnp.bfloat16)
    mixture = jnp.einsum(
        "kgts,skd->tkgd", weights, value_three, preferred_element_type=jnp.float32
    )
    return mixture.astype(jnp.bfloat16).reshape(rows.shape[0], queries.shape[1])


def swap_cores(piece):
    return lax.ppermute(piece, CORE, [(0, 1), (1, 0)])


def gather_marks(query_marks, output_marks):
    core = lax.axis_index(CORE)
    own = jnp.stack([query_marks, output_marks])
    other = swap_cores(own)
    first = core == 0
    pair = jnp.where(first, jnp.stack([own, other], 1), jnp.stack([other, own], 1))
    mine = jnp.where(first, pair[0], pair[1])
    fetched = broadcast_gather(mine, CHIPS)
    swapped = swap_cores(fetched)
    query_rows = jnp.where(first, fetched, swapped)
    output_rows = jnp.where(first, swapped, fetched)
    return jnp.stack([query_rows, output_rows])


def broadcast_gather(piece, axis_name):
    count = lax.axis_size(axis_name)
    spread = jnp.broadcast_to(piece[None], (count,) + piece.shape)
    return lax.all_to_all(spread, axis_name, 0, 0, tiled=True)


def shards(queries, key_rows, value_rows, landmark_index, radius_in, radius_out):
    length = queries.shape[0]
    model_count = lax.axis_size(MODEL)
    data_count = lax.axis_size(DATA)
    model_index = lax.axis_index(MODEL)
    landmarks = radius_in.shape[0]
    row_share = landmarks // model_count
    column_share = landmarks // data_count
    token_count = length * data_count

    own_rows = landmark_index % length
    gathered = gather_marks(
        jnp.take(queries, own_rows, axis=0),
        attend_rows(queries, key_rows, value_rows, own_rows),
    )
    landmark_piece = gathered.reshape(2, landmarks, queries.shape[1])
    attended = attend(queries, key_rows, value_rows)

    row_norms = jnp.stack([squares_by_row(queries), squares_by_row(attended)])
    mark_norms = squares_by_row(landmark_piece)
    cross = jnp.stack(
        [inner_rows(queries, landmark_piece[0]), inner_rows(attended, landmark_piece[1])]
    )
    distance_part = row_norms[:, :, None] + mark_norms[:, None, :] - 2.0 * cross
    distance_part = distance_part.reshape(2, length, model_count, row_share)
    distance = jnp.sum(
        lax.all_to_all(distance_part, MODEL, 2, 2, tiled=True), axis=2
    )

    widths = lax.dynamic_slice_in_dim(
        jnp.stack([radius_in, radius_out]), model_index * row_share, row_share, 1
    )
    features = jnp.exp(-distance / (D * widths[:, None, :])).astype(jnp.bfloat16)
    row_features = features[0]
    column_features = jnp.transpose(
        broadcast_gather(features[1], MODEL), (1, 0, 2)
    ).reshape(length, landmarks)

    rows32 = row_features.astype(jnp.float32)
    columns32 = column_features.astype(jnp.float32)
    row_mean = jnp.mean(rows32, axis=0)
    column_mean = jnp.mean(columns32, axis=0)
    rows_centered = rows32 - row_mean[None, :]
    columns_centered = columns32 - column_mean[None, :]
    second = lax.dot_general(
        rows_centered,
        columns_centered,
        (((0,), (0,)), ((), ())),
        precision=lax.Precision.HIGHEST,
        preferred_element_type=jnp.float32,
    )
    row_square = jnp.sum(jnp.square(rows_centered), axis=0)
    column_square = jnp.sum(jnp.square(columns_centered), axis=0)

    stats = (second, row_mean, row_square, column_mean, column_square)
    stats = exchange_merge(stats, "z", 8, length)
    stats = exchange_merge(stats, ("y_hi", CORE), 8, 8 * length)
    second, row_mean, row_square, column_mean, column_square = stats
    return second / token_count / jnp.sqrt(
        (row_square / token_count + EPSILON)[:, None]
        * (column_square / token_count + EPSILON)[None, :]
    )


def exchange_merge(stats, axis_name, count, group_tokens):
    second, row_mean, row_square, column_mean, column_square = stats
    rows, columns = second.shape
    share = columns // count
    packed = jnp.concatenate(
        [
            jnp.transpose(second.reshape(rows, count, share), (1, 0, 2)).reshape(
                count, rows * share
            ),
            jnp.broadcast_to(row_mean[None], (count, rows)),
            jnp.broadcast_to(row_square[None], (count, rows)),
            column_mean.reshape(count, share),
            column_square.reshape(count, share),
        ],
        axis=1,
    )
    received = lax.all_to_all(packed, axis_name, 0, 0, tiled=True)
    cut = rows * share
    seconds = received[:, :cut].reshape(count, rows, share)
    row_means = received[:, cut : cut + rows]
    row_squares = received[:, cut + rows : cut + 2 * rows]
    column_means = received[:, cut + 2 * rows : cut + 2 * rows + share]
    column_squares = received[:, cut + 2 * rows + share :]
    row_total = jnp.mean(row_means, axis=0)
    column_total = jnp.mean(column_means, axis=0)
    row_shift = row_means - row_total[None, :]
    column_shift = column_means - column_total[None, :]
    between = jnp.sum(row_shift[:, :, None] * column_shift[:, None, :], axis=0)
    return (
        jnp.sum(seconds, axis=0) + group_tokens * between,
        row_total,
        jnp.sum(row_squares, axis=0) + group_tokens * jnp.sum(jnp.square(row_shift), axis=0),
        column_total,
        jnp.sum(column_squares, axis=0)
        + group_tokens * jnp.sum(jnp.square(column_shift), axis=0),
    )


def solution(mesh):
    data_count, model_count = mesh.devices.shape
    chips = mesh.devices.reshape(data_count // 8, 4, 2, model_count // 2, 2)
    split = Mesh(chips, DATA + MODEL)
    return jax.shard_map(
        shards,
        mesh=split,
        in_specs=(P(DATA, MODEL), P(DATA, MODEL), P(DATA, MODEL), P(DATA), P(), P()),
        out_specs=P(MODEL, DATA),
        check_vma=False,
    )
```

```python
import math

import jax
import jax.numpy as jnp
from jax import lax
from jax.sharding import Mesh, PartitionSpec as P

D = 8192
HEAD_DIM = 128


EPSILON = 1e-06

CHIPS = ("z", "y_hi")
CORE = "core"
DATA = CHIPS + (CORE,)
MODEL = ("x", "y_lo")


def attend(queries, key_rows, value_rows):
    length = queries.shape[0]
    kv_heads = key_rows.shape[1] // HEAD_DIM
    group_size = queries.shape[1] // HEAD_DIM // kv_heads
    query_four = queries.reshape(length, kv_heads, group_size, HEAD_DIM)
    key_three = key_rows.reshape(length, kv_heads, HEAD_DIM)
    value_three = value_rows.reshape(length, kv_heads, HEAD_DIM)
    scores = jnp.einsum(
        "tkgd,skd->kgts", query_four, key_three, preferred_element_type=jnp.float32
    ) / math.sqrt(HEAD_DIM)
    row_position = lax.broadcasted_iota(jnp.int32, (length, length), 0)
    column_position = lax.broadcasted_iota(jnp.int32, (length, length), 1)
    scores = jnp.where(column_position <= row_position, scores, -jnp.inf)
    weights = jax.nn.softmax(scores, axis=-1).astype(jnp.bfloat16)
    mixture = jnp.einsum(
        "kgts,skd->tkgd", weights, value_three, preferred_element_type=jnp.float32
    )
    return mixture.astype(jnp.bfloat16).reshape(length, queries.shape[1])


def squares_by_row(matrix):
    return jnp.sum(jnp.square(matrix.astype(jnp.float32)), axis=-1)


def inner_rows(left, right):
    return lax.dot_general(
        left, right, (((1,), (1,)), ((), ())), preferred_element_type=jnp.float32
    )


def attend_rows(queries, key_rows, value_rows, rows):
    length = queries.shape[0]
    kv_heads = key_rows.shape[1] // HEAD_DIM
    group_size = queries.shape[1] // HEAD_DIM // kv_heads
    picked = jnp.take(queries, rows, axis=0)
    query_four = picked.reshape(rows.shape[0], kv_heads, group_size, HEAD_DIM)
    key_three = key_rows.reshape(length, kv_heads, HEAD_DIM)
    value_three = value_rows.reshape(length, kv_heads, HEAD_DIM)
    scores = jnp.einsum(
        "tkgd,skd->kgts", query_four, key_three, preferred_element_type=jnp.float32
    ) / math.sqrt(HEAD_DIM)
    column_position = lax.broadcasted_iota(jnp.int32, (rows.shape[0], length), 1)
    scores = jnp.where(column_position <= rows[:, None], scores, -jnp.inf)
    weights = jax.nn.softmax(scores, axis=-1).astype(jnp.bfloat16)
    mixture = jnp.einsum(
        "kgts,skd->tkgd", weights, value_three, preferred_element_type=jnp.float32
    )
    return mixture.astype(jnp.bfloat16).reshape(rows.shape[0], queries.shape[1])


def swap_cores(piece):
    return lax.ppermute(piece, CORE, [(0, 1), (1, 0)])


def gather_marks(query_marks, output_marks):
    core = lax.axis_index(CORE)
    own = jnp.stack([query_marks, output_marks])
    other = swap_cores(own)
    first = core == 0
    pair = jnp.where(first, jnp.stack([own, other], 1), jnp.stack([other, own], 1))
    mine = jnp.where(first, pair[0], pair[1])
    fetched = broadcast_gather(mine, CHIPS)
    return fetched.reshape((-1,) + fetched.shape[3:])


def partial_distance(rows, marks):
    return (
        squares_by_row(rows)[:, None]
        + squares_by_row(marks)[None, :]
        - 2.0 * inner_rows(rows, marks)
    )


def broadcast_gather(piece, axis_name):
    count = lax.axis_size(axis_name)
    spread = jnp.broadcast_to(piece[None], (count,) + piece.shape)
    return lax.all_to_all(spread, axis_name, 0, 0, tiled=True)


def shards(queries, key_rows, value_rows, landmark_index, radius_in, radius_out):
    length = queries.shape[0]
    model_count = lax.axis_size(MODEL)
    data_count = lax.axis_size(DATA)
    model_index = lax.axis_index(MODEL)
    landmarks = radius_in.shape[0]
    row_share = landmarks // model_count
    column_share = landmarks // data_count
    token_count = length * data_count

    own_rows = landmark_index % length
    first = lax.axis_index(CORE) == 0
    fetched = gather_marks(
        jnp.take(queries, own_rows, axis=0),
        attend_rows(queries, key_rows, value_rows, own_rows),
    )
    swapped = swap_cores(fetched)
    attended = attend(queries, key_rows, value_rows)
    fetched_part = partial_distance(jnp.where(first, queries, attended), fetched)
    swapped_part = partial_distance(jnp.where(first, attended, queries), swapped)
    distance_part = jnp.where(
        first,
        jnp.stack([fetched_part, swapped_part]),
        jnp.stack([swapped_part, fetched_part]),
    )
    distance_part = distance_part.reshape(2, length, model_count, row_share)
    distance = jnp.sum(
        lax.all_to_all(distance_part, MODEL, 2, 2, tiled=True), axis=2
    )

    widths = lax.dynamic_slice_in_dim(
        jnp.stack([radius_in, radius_out]), model_index * row_share, row_share, 1
    )
    features = jnp.exp(-distance / (D * widths[:, None, :])).astype(jnp.bfloat16)
    row_features = features[0]
    column_features = jnp.transpose(
        broadcast_gather(features[1], MODEL), (1, 0, 2)
    ).reshape(length, landmarks)

    rows32 = row_features.astype(jnp.float32)
    columns32 = column_features.astype(jnp.float32)
    row_mean = jnp.mean(rows32, axis=0)
    column_mean = jnp.mean(columns32, axis=0)
    rows_centered = rows32 - row_mean[None, :]
    columns_centered = columns32 - column_mean[None, :]
    second = lax.dot_general(
        rows_centered,
        columns_centered,
        (((0,), (0,)), ((), ())),
        precision=lax.Precision.HIGHEST,
        preferred_element_type=jnp.float32,
    )
    row_square = jnp.sum(jnp.square(rows_centered), axis=0)
    column_square = jnp.sum(jnp.square(columns_centered), axis=0)

    packed = jnp.concatenate(
        [
            jnp.transpose(
                second.reshape(row_share, data_count, column_share), (1, 0, 2)
            ).reshape(data_count, row_share * column_share),
            jnp.broadcast_to(row_mean[None], (data_count, row_share)),
            jnp.broadcast_to(row_square[None], (data_count, row_share)),
            column_mean.reshape(data_count, column_share),
            column_square.reshape(data_count, column_share),
        ],
        axis=1,
    )
    received = lax.all_to_all(packed, DATA, 0, 0, tiled=True)
    cut = row_share * column_share
    second_parts = received[:, :cut].reshape(data_count, row_share, column_share)
    row_means = received[:, cut : cut + row_share]
    row_squares = received[:, cut + row_share : cut + 2 * row_share]
    column_means = received[:, cut + 2 * row_share : cut + 2 * row_share + column_share]
    column_squares = received[:, cut + 2 * row_share + column_share :]

    row_shift = row_means - jnp.mean(row_means, axis=0)[None, :]
    column_shift = column_means - jnp.mean(column_means, axis=0)[None, :]
    between = jnp.sum(row_shift[:, :, None] * column_shift[:, None, :], axis=0)
    covariance = (jnp.sum(second_parts, axis=0) + length * between) / token_count
    spread_rows = (
        jnp.sum(row_squares, axis=0) + length * jnp.sum(jnp.square(row_shift), axis=0)
    ) / token_count
    spread_columns = (
        jnp.sum(column_squares, axis=0)
        + length * jnp.sum(jnp.square(column_shift), axis=0)
    ) / token_count
    return covariance / jnp.sqrt(
        (spread_rows + EPSILON)[:, None] * (spread_columns + EPSILON)[None, :]
    )


def solution(mesh):
    data_count, model_count = mesh.devices.shape
    chips = mesh.devices.reshape(data_count // 8, 4, 2, model_count // 2, 2)
    split = Mesh(chips, DATA + MODEL)
    return jax.shard_map(
        shards,
        mesh=split,
        in_specs=(P(DATA, MODEL), P(DATA, MODEL), P(DATA, MODEL), P(DATA), P(), P()),
        out_specs=P(MODEL, DATA),
        check_vma=False,
    )
```

```python
import math

import jax
import jax.numpy as jnp
from jax import lax
from jax.sharding import Mesh, PartitionSpec as P

D = 8192
HEAD_DIM = 128


EPSILON = 1e-06

CHIPS = ("z", "y_hi")
CORE = "core"
DATA = CHIPS + (CORE,)
MODEL = ("x", "y_lo")


def attend(queries, key_rows, value_rows):
    length = queries.shape[0]
    kv_heads = key_rows.shape[1] // HEAD_DIM
    group_size = queries.shape[1] // HEAD_DIM // kv_heads
    query_four = queries.reshape(length, kv_heads, group_size, HEAD_DIM)
    key_three = key_rows.reshape(length, kv_heads, HEAD_DIM)
    value_three = value_rows.reshape(length, kv_heads, HEAD_DIM)
    scores = jnp.einsum(
        "tkgd,skd->kgts", query_four, key_three, preferred_element_type=jnp.float32
    ) / math.sqrt(HEAD_DIM)
    row_position = lax.broadcasted_iota(jnp.int32, (length, length), 0)
    column_position = lax.broadcasted_iota(jnp.int32, (length, length), 1)
    scores = jnp.where(column_position <= row_position, scores, -jnp.inf)
    weights = jax.nn.softmax(scores, axis=-1).astype(jnp.bfloat16)
    mixture = jnp.einsum(
        "kgts,skd->tkgd", weights, value_three, preferred_element_type=jnp.float32
    )
    return mixture.astype(jnp.bfloat16).reshape(length, queries.shape[1])


def squares_by_row(matrix):
    return jnp.sum(jnp.square(matrix.astype(jnp.float32)), axis=-1)


def inner_rows(left, right):
    return lax.dot_general(
        left, right, (((1,), (1,)), ((), ())), preferred_element_type=jnp.float32
    )


def attend_rows(queries, key_rows, value_rows, rows):
    length = queries.shape[0]
    kv_heads = key_rows.shape[1] // HEAD_DIM
    group_size = queries.shape[1] // HEAD_DIM // kv_heads
    picked = jnp.take(queries, rows, axis=0)
    query_four = picked.reshape(rows.shape[0], kv_heads, group_size, HEAD_DIM)
    key_three = key_rows.reshape(length, kv_heads, HEAD_DIM)
    value_three = value_rows.reshape(length, kv_heads, HEAD_DIM)
    scores = jnp.einsum(
        "tkgd,skd->kgts", query_four, key_three, preferred_element_type=jnp.float32
    ) / math.sqrt(HEAD_DIM)
    column_position = lax.broadcasted_iota(jnp.int32, (rows.shape[0], length), 1)
    scores = jnp.where(column_position <= rows[:, None], scores, -jnp.inf)
    weights = jax.nn.softmax(scores, axis=-1).astype(jnp.bfloat16)
    mixture = jnp.einsum(
        "kgts,skd->tkgd", weights, value_three, preferred_element_type=jnp.float32
    )
    return mixture.astype(jnp.bfloat16).reshape(rows.shape[0], queries.shape[1])


def swap_cores(piece):
    return lax.ppermute(piece, CORE, [(0, 1), (1, 0)])


def gather_marks(query_marks, output_marks):
    first = lax.axis_index(CORE) == 0
    data_count = lax.axis_size(DATA)
    kinds = jnp.stack([query_marks, output_marks])
    spread = jnp.broadcast_to(kinds[None], (data_count // 2,) + kinds.shape)
    fetched = lax.all_to_all(
        spread.reshape((data_count,) + query_marks.shape), DATA, 0, 0, tiled=True
    )
    swapped = swap_cores(fetched)
    query_rows = jnp.where(first, fetched, swapped)
    output_rows = jnp.where(first, swapped, fetched)
    return jnp.stack([query_rows, output_rows])


def broadcast_gather(piece, axis_name):
    count = lax.axis_size(axis_name)
    spread = jnp.broadcast_to(piece[None], (count,) + piece.shape)
    return lax.all_to_all(spread, axis_name, 0, 0, tiled=True)


def shards(queries, key_rows, value_rows, landmark_index, radius_in, radius_out):
    length = queries.shape[0]
    model_count = lax.axis_size(MODEL)
    data_count = lax.axis_size(DATA)
    model_index = lax.axis_index(MODEL)
    landmarks = radius_in.shape[0]
    row_share = landmarks // model_count
    column_share = landmarks // data_count
    token_count = length * data_count

    own_rows = landmark_index % length
    gathered = gather_marks(
        jnp.take(queries, own_rows, axis=0),
        attend_rows(queries, key_rows, value_rows, own_rows),
    )
    landmark_piece = gathered.reshape(2, landmarks, queries.shape[1])
    attended = attend(queries, key_rows, value_rows)

    row_norms = jnp.stack([squares_by_row(queries), squares_by_row(attended)])
    mark_norms = squares_by_row(landmark_piece)
    cross = jnp.stack(
        [inner_rows(queries, landmark_piece[0]), inner_rows(attended, landmark_piece[1])]
    )
    distance_part = row_norms[:, :, None] + mark_norms[:, None, :] - 2.0 * cross
    distance_part = distance_part.reshape(2, length, model_count, row_share)
    distance = jnp.sum(
        lax.all_to_all(distance_part, MODEL, 2, 2, tiled=True), axis=2
    )

    widths = lax.dynamic_slice_in_dim(
        jnp.stack([radius_in, radius_out]), model_index * row_share, row_share, 1
    )
    features = jnp.exp(-distance / (D * widths[:, None, :])).astype(jnp.bfloat16)
    row_features = features[0]
    column_features = jnp.transpose(
        broadcast_gather(features[1], MODEL), (1, 0, 2)
    ).reshape(length, landmarks)

    rows32 = row_features.astype(jnp.float32)
    columns32 = column_features.astype(jnp.float32)
    row_mean = jnp.mean(rows32, axis=0)
    column_mean = jnp.mean(columns32, axis=0)
    rows_centered = rows32 - row_mean[None, :]
    columns_centered = columns32 - column_mean[None, :]
    second = lax.dot_general(
        rows_centered,
        columns_centered,
        (((0,), (0,)), ((), ())),
        precision=lax.Precision.HIGHEST,
        preferred_element_type=jnp.float32,
    )
    row_square = jnp.sum(jnp.square(rows_centered), axis=0)
    column_square = jnp.sum(jnp.square(columns_centered), axis=0)

    packed = jnp.concatenate(
        [
            jnp.transpose(
                second.reshape(row_share, data_count, column_share), (1, 0, 2)
            ).reshape(data_count, row_share * column_share),
            jnp.broadcast_to(row_mean[None], (data_count, row_share)),
            jnp.broadcast_to(row_square[None], (data_count, row_share)),
            column_mean.reshape(data_count, column_share),
            column_square.reshape(data_count, column_share),
        ],
        axis=1,
    )
    received = lax.all_to_all(packed, DATA, 0, 0, tiled=True)
    cut = row_share * column_share
    second_parts = received[:, :cut].reshape(data_count, row_share, column_share)
    row_means = received[:, cut : cut + row_share]
    row_squares = received[:, cut + row_share : cut + 2 * row_share]
    column_means = received[:, cut + 2 * row_share : cut + 2 * row_share + column_share]
    column_squares = received[:, cut + 2 * row_share + column_share :]

    row_shift = row_means - jnp.mean(row_means, axis=0)[None, :]
    column_shift = column_means - jnp.mean(column_means, axis=0)[None, :]
    between = jnp.sum(row_shift[:, :, None] * column_shift[:, None, :], axis=0)
    covariance = (jnp.sum(second_parts, axis=0) + length * between) / token_count
    spread_rows = (
        jnp.sum(row_squares, axis=0) + length * jnp.sum(jnp.square(row_shift), axis=0)
    ) / token_count
    spread_columns = (
        jnp.sum(column_squares, axis=0)
        + length * jnp.sum(jnp.square(column_shift), axis=0)
    ) / token_count
    return covariance / jnp.sqrt(
        (spread_rows + EPSILON)[:, None] * (spread_columns + EPSILON)[None, :]
    )


def solution(mesh):
    data_count, model_count = mesh.devices.shape
    chips = mesh.devices.reshape(data_count // 8, 4, 2, model_count // 2, 2)
    split = Mesh(chips, DATA + MODEL)
    return jax.shard_map(
        shards,
        mesh=split,
        in_specs=(P(DATA, MODEL), P(DATA, MODEL), P(DATA, MODEL), P(DATA), P(), P()),
        out_specs=P(MODEL, DATA),
        check_vma=False,
    )
```

```python
import math

import jax
import jax.numpy as jnp
from jax import lax
from jax.sharding import Mesh, PartitionSpec as P

D = 8192
HEAD_DIM = 128


EPSILON = 1e-06

CHIPS = ("z", "y_hi")
CORE = "core"
DATA = CHIPS + (CORE,)
MODEL = ("x", "y_lo")


def attend(queries, key_rows, value_rows):
    length = queries.shape[0]
    kv_heads = key_rows.shape[1] // HEAD_DIM
    group_size = queries.shape[1] // HEAD_DIM // kv_heads
    query_four = queries.reshape(length, kv_heads, group_size, HEAD_DIM)
    key_three = key_rows.reshape(length, kv_heads, HEAD_DIM)
    value_three = value_rows.reshape(length, kv_heads, HEAD_DIM)
    scores = jnp.einsum(
        "tkgd,skd->kgts", query_four, key_three, preferred_element_type=jnp.float32
    ) / math.sqrt(HEAD_DIM)
    row_position = lax.broadcasted_iota(jnp.int32, (length, length), 0)
    column_position = lax.broadcasted_iota(jnp.int32, (length, length), 1)
    scores = jnp.where(column_position <= row_position, scores, -jnp.inf)
    weights = jax.nn.softmax(scores, axis=-1).astype(jnp.bfloat16)
    mixture = jnp.einsum(
        "kgts,skd->tkgd", weights, value_three, preferred_element_type=jnp.float32
    )
    return mixture.astype(jnp.bfloat16).reshape(length, queries.shape[1])


def squares_by_row(matrix):
    return jnp.sum(jnp.square(matrix.astype(jnp.float32)), axis=-1)


def inner_rows(left, right):
    return lax.dot_general(
        left, right, (((1,), (1,)), ((), ())), preferred_element_type=jnp.float32
    )


def attend_rows(queries, key_rows, value_rows, rows):
    length = queries.shape[0]
    kv_heads = key_rows.shape[1] // HEAD_DIM
    group_size = queries.shape[1] // HEAD_DIM // kv_heads
    picked = pick_rows(queries, rows)
    query_four = picked.reshape(rows.shape[0], kv_heads, group_size, HEAD_DIM)
    key_three = key_rows.reshape(length, kv_heads, HEAD_DIM)
    value_three = value_rows.reshape(length, kv_heads, HEAD_DIM)
    scores = jnp.einsum(
        "tkgd,skd->kgts", query_four, key_three, preferred_element_type=jnp.float32
    ) / math.sqrt(HEAD_DIM)
    column_position = lax.broadcasted_iota(jnp.int32, (rows.shape[0], length), 1)
    scores = jnp.where(column_position <= rows[:, None], scores, -jnp.inf)
    weights = jax.nn.softmax(scores, axis=-1).astype(jnp.bfloat16)
    mixture = jnp.einsum(
        "kgts,skd->tkgd", weights, value_three, preferred_element_type=jnp.float32
    )
    return mixture.astype(jnp.bfloat16).reshape(rows.shape[0], queries.shape[1])


def pick_rows(matrix, rows):
    hits = rows[:, None] == lax.broadcasted_iota(jnp.int32, (rows.shape[0], matrix.shape[0]), 1)
    return jnp.dot(
        hits.astype(matrix.dtype), matrix, preferred_element_type=jnp.float32
    ).astype(matrix.dtype)


def swap_cores(piece):
    return lax.ppermute(piece, CORE, [(0, 1), (1, 0)])


def gather_marks(query_marks, output_marks):
    first = lax.axis_index(CORE) == 0
    data_count = lax.axis_size(DATA)
    kinds = jnp.stack([query_marks, output_marks])
    spread = jnp.broadcast_to(kinds[None], (data_count // 2,) + kinds.shape)
    fetched = lax.all_to_all(
        spread.reshape((data_count,) + query_marks.shape), DATA, 0, 0, tiled=True
    )
    swapped = swap_cores(fetched)
    query_rows = jnp.where(first, fetched, swapped)
    output_rows = jnp.where(first, swapped, fetched)
    return jnp.stack([query_rows, output_rows])


def broadcast_gather(piece, axis_name):
    count = lax.axis_size(axis_name)
    spread = jnp.broadcast_to(piece[None], (count,) + piece.shape)
    return lax.all_to_all(spread, axis_name, 0, 0, tiled=True)


def shards(queries, key_rows, value_rows, landmark_index, radius_in, radius_out):
    length = queries.shape[0]
    model_count = lax.axis_size(MODEL)
    data_count = lax.axis_size(DATA)
    model_index = lax.axis_index(MODEL)
    landmarks = radius_in.shape[0]
    row_share = landmarks // model_count
    column_share = landmarks // data_count
    token_count = length * data_count

    own_rows = landmark_index % length
    gathered = gather_marks(
        pick_rows(queries, own_rows),
        attend_rows(queries, key_rows, value_rows, own_rows),
    )
    landmark_piece = gathered.reshape(2, landmarks, queries.shape[1])
    attended = attend(queries, key_rows, value_rows)

    row_norms = jnp.stack([squares_by_row(queries), squares_by_row(attended)])
    mark_norms = squares_by_row(landmark_piece)
    cross = jnp.stack(
        [inner_rows(landmark_piece[0], queries), inner_rows(landmark_piece[1], attended)]
    )
    distance_part = mark_norms[:, :, None] + row_norms[:, None, :] - 2.0 * cross
    distance_part = jnp.transpose(
        distance_part.reshape(2, model_count, row_share, length), (1, 0, 2, 3)
    )
    distance = jnp.sum(
        lax.all_to_all(distance_part, MODEL, 0, 0, tiled=True), axis=0
    )

    widths = lax.dynamic_slice_in_dim(
        jnp.stack([radius_in, radius_out]), model_index * row_share, row_share, 1
    )
    features = jnp.exp(-distance / (D * widths[:, :, None])).astype(jnp.bfloat16)
    row_features = features[0]
    column_features = broadcast_gather(features[1], MODEL).reshape(landmarks, length)

    rows32 = row_features.astype(jnp.float32)
    columns32 = column_features.astype(jnp.float32)
    row_mean = jnp.mean(rows32, axis=1)
    column_mean = jnp.mean(columns32, axis=1)
    rows_centered = rows32 - row_mean[:, None]
    columns_centered = columns32 - column_mean[:, None]
    second = lax.dot_general(
        rows_centered,
        columns_centered,
        (((1,), (1,)), ((), ())),
        precision=lax.Precision.HIGHEST,
        preferred_element_type=jnp.float32,
    )
    row_square = jnp.sum(jnp.square(rows_centered), axis=1)
    column_square = jnp.sum(jnp.square(columns_centered), axis=1)

    packed = jnp.concatenate(
        [
            jnp.transpose(
                second.reshape(row_share, data_count, column_share), (1, 0, 2)
            ).reshape(data_count, row_share * column_share),
            jnp.broadcast_to(row_mean[None], (data_count, row_share)),
            jnp.broadcast_to(row_square[None], (data_count, row_share)),
            column_mean.reshape(data_count, column_share),
            column_square.reshape(data_count, column_share),
        ],
        axis=1,
    )
    received = lax.all_to_all(packed, DATA, 0, 0, tiled=True)
    cut = row_share * column_share
    second_parts = received[:, :cut].reshape(data_count, row_share, column_share)
    row_means = received[:, cut : cut + row_share]
    row_squares = received[:, cut + row_share : cut + 2 * row_share]
    column_means = received[:, cut + 2 * row_share : cut + 2 * row_share + column_share]
    column_squares = received[:, cut + 2 * row_share + column_share :]

    row_shift = row_means - jnp.mean(row_means, axis=0)[None, :]
    column_shift = column_means - jnp.mean(column_means, axis=0)[None, :]
    between = jnp.sum(row_shift[:, :, None] * column_shift[:, None, :], axis=0)
    covariance = (jnp.sum(second_parts, axis=0) + length * between) / token_count
    spread_rows = (
        jnp.sum(row_squares, axis=0) + length * jnp.sum(jnp.square(row_shift), axis=0)
    ) / token_count
    spread_columns = (
        jnp.sum(column_squares, axis=0)
        + length * jnp.sum(jnp.square(column_shift), axis=0)
    ) / token_count
    return covariance / jnp.sqrt(
        (spread_rows + EPSILON)[:, None] * (spread_columns + EPSILON)[None, :]
    )


def solution(mesh):
    data_count, model_count = mesh.devices.shape
    chips = mesh.devices.reshape(data_count // 8, 4, 2, model_count // 2, 2)
    split = Mesh(chips, DATA + MODEL)
    return jax.shard_map(
        shards,
        mesh=split,
        in_specs=(P(DATA, MODEL), P(DATA, MODEL), P(DATA, MODEL), P(DATA), P(), P()),
        out_specs=P(MODEL, DATA),
        check_vma=False,
    )
```

```python
import math

import jax
import jax.numpy as jnp
from jax import lax
from jax.sharding import Mesh, PartitionSpec as P

D = 8192
HEAD_DIM = 128


EPSILON = 1e-06

CHIPS = ("z", "y_hi")
CORE = "core"
DATA = CHIPS + (CORE,)
MODEL = ("x", "y_lo")


def attend(queries, key_rows, value_rows):
    length = queries.shape[0]
    kv_heads = key_rows.shape[1] // HEAD_DIM
    group_size = queries.shape[1] // HEAD_DIM // kv_heads
    query_four = queries.reshape(length, kv_heads, group_size, HEAD_DIM)
    key_three = key_rows.reshape(length, kv_heads, HEAD_DIM)
    value_three = value_rows.reshape(length, kv_heads, HEAD_DIM)
    scores = jnp.einsum(
        "tkgd,skd->kgts", query_four, key_three, preferred_element_type=jnp.float32
    ) / math.sqrt(HEAD_DIM)
    row_position = lax.broadcasted_iota(jnp.int32, (length, length), 0)
    column_position = lax.broadcasted_iota(jnp.int32, (length, length), 1)
    scores = jnp.where(column_position <= row_position, scores, -jnp.inf)
    weights = jax.nn.softmax(scores, axis=-1).astype(jnp.bfloat16)
    mixture = jnp.einsum(
        "kgts,skd->tkgd", weights, value_three, preferred_element_type=jnp.float32
    )
    return mixture.astype(jnp.bfloat16).reshape(length, queries.shape[1])


def squares_by_row(matrix):
    return jnp.sum(jnp.square(matrix.astype(jnp.float32)), axis=-1)


def inner_rows(left, right):
    return lax.dot_general(
        left, right, (((1,), (1,)), ((), ())), preferred_element_type=jnp.float32
    )


def attend_rows(queries, key_rows, value_rows, rows):
    length = queries.shape[0]
    kv_heads = key_rows.shape[1] // HEAD_DIM
    group_size = queries.shape[1] // HEAD_DIM // kv_heads
    picked = pick_rows(queries, rows)
    query_four = picked.reshape(rows.shape[0], kv_heads, group_size, HEAD_DIM)
    key_three = key_rows.reshape(length, kv_heads, HEAD_DIM)
    value_three = value_rows.reshape(length, kv_heads, HEAD_DIM)
    scores = jnp.einsum(
        "tkgd,skd->kgts", query_four, key_three, preferred_element_type=jnp.float32
    ) / math.sqrt(HEAD_DIM)
    column_position = lax.broadcasted_iota(jnp.int32, (rows.shape[0], length), 1)
    scores = jnp.where(column_position <= rows[:, None], scores, -jnp.inf)
    weights = jax.nn.softmax(scores, axis=-1).astype(jnp.bfloat16)
    mixture = jnp.einsum(
        "kgts,skd->tkgd", weights, value_three, preferred_element_type=jnp.float32
    )
    return mixture.astype(jnp.bfloat16).reshape(rows.shape[0], queries.shape[1])


def pick_rows(matrix, rows):
    hits = rows[:, None] == lax.broadcasted_iota(jnp.int32, (rows.shape[0], matrix.shape[0]), 1)
    return jnp.dot(
        hits.astype(matrix.dtype), matrix, preferred_element_type=jnp.float32
    ).astype(matrix.dtype)


def swap_cores(piece):
    return lax.ppermute(piece, CORE, [(0, 1), (1, 0)])


def gather_marks(query_marks, output_marks):
    data_count = lax.axis_size(DATA)
    kinds = jnp.stack([query_marks, output_marks])
    spread = jnp.broadcast_to(kinds[None], (data_count // 2,) + kinds.shape)
    return lax.all_to_all(
        spread.reshape((data_count,) + query_marks.shape), DATA, 0, 0, tiled=True
    )


def broadcast_gather(piece, axis_name):
    count = lax.axis_size(axis_name)
    spread = jnp.broadcast_to(piece[None], (count,) + piece.shape)
    return lax.all_to_all(spread, axis_name, 0, 0, tiled=True)


def shards(queries, key_rows, value_rows, landmark_index, radius_in, radius_out):
    length = queries.shape[0]
    model_count = lax.axis_size(MODEL)
    data_count = lax.axis_size(DATA)
    model_index = lax.axis_index(MODEL)
    landmarks = radius_in.shape[0]
    row_share = landmarks // model_count
    column_share = landmarks // data_count
    token_count = length * data_count

    own_rows = landmark_index % length
    first = lax.axis_index(CORE) == 0
    marks = gather_marks(
        pick_rows(queries, own_rows),
        attend_rows(queries, key_rows, value_rows, own_rows),
    ).reshape(landmarks, queries.shape[1])
    attended = attend(queries, key_rows, value_rows)
    own_side = jnp.where(first, queries, attended)
    other_side = swap_cores(jnp.where(first, attended, queries))
    tokens = jnp.stack([own_side, other_side])

    row_norms = squares_by_row(tokens)
    mark_norms = squares_by_row(marks)
    cross = jnp.stack([inner_rows(marks, tokens[0]), inner_rows(marks, tokens[1])])
    distance_part = mark_norms[None, :, None] + row_norms[:, None, :] - 2.0 * cross
    distance_part = jnp.transpose(
        distance_part.reshape(2, model_count, row_share, length), (1, 0, 2, 3)
    )
    distance = jnp.sum(
        lax.all_to_all(distance_part, MODEL, 0, 0, tiled=True), axis=0
    )

    radius = jnp.where(first, radius_in, radius_out)
    widths = lax.dynamic_slice_in_dim(radius, model_index * row_share, row_share, 0)
    side = jnp.exp(-distance / (D * widths[None, :, None])).astype(jnp.bfloat16)
    handed = swap_cores(side[1])
    row_features = jnp.where(first, side[0], handed)
    own_columns = jnp.where(first, handed, side[0])
    column_features = broadcast_gather(own_columns, MODEL).reshape(landmarks, length)

    rows32 = row_features.astype(jnp.float32)
    columns32 = column_features.astype(jnp.float32)
    row_mean = jnp.mean(rows32, axis=1)
    column_mean = jnp.mean(columns32, axis=1)
    rows_centered = rows32 - row_mean[:, None]
    columns_centered = columns32 - column_mean[:, None]
    second = lax.dot_general(
        rows_centered,
        columns_centered,
        (((1,), (1,)), ((), ())),
        precision=lax.Precision.HIGHEST,
        preferred_element_type=jnp.float32,
    )
    row_square = jnp.sum(jnp.square(rows_centered), axis=1)
    column_square = jnp.sum(jnp.square(columns_centered), axis=1)

    packed = jnp.concatenate(
        [
            jnp.transpose(
                second.reshape(row_share, data_count, column_share), (1, 0, 2)
            ).reshape(data_count, row_share * column_share),
            jnp.broadcast_to(row_mean[None], (data_count, row_share)),
            jnp.broadcast_to(row_square[None], (data_count, row_share)),
            column_mean.reshape(data_count, column_share),
            column_square.reshape(data_count, column_share),
        ],
        axis=1,
    )
    received = lax.all_to_all(packed, DATA, 0, 0, tiled=True)
    cut = row_share * column_share
    second_parts = received[:, :cut].reshape(data_count, row_share, column_share)
    row_means = received[:, cut : cut + row_share]
    row_squares = received[:, cut + row_share : cut + 2 * row_share]
    column_means = received[:, cut + 2 * row_share : cut + 2 * row_share + column_share]
    column_squares = received[:, cut + 2 * row_share + column_share :]

    row_shift = row_means - jnp.mean(row_means, axis=0)[None, :]
    column_shift = column_means - jnp.mean(column_means, axis=0)[None, :]
    between = jnp.sum(row_shift[:, :, None] * column_shift[:, None, :], axis=0)
    covariance = (jnp.sum(second_parts, axis=0) + length * between) / token_count
    spread_rows = (
        jnp.sum(row_squares, axis=0) + length * jnp.sum(jnp.square(row_shift), axis=0)
    ) / token_count
    spread_columns = (
        jnp.sum(column_squares, axis=0)
        + length * jnp.sum(jnp.square(column_shift), axis=0)
    ) / token_count
    return covariance / jnp.sqrt(
        (spread_rows + EPSILON)[:, None] * (spread_columns + EPSILON)[None, :]
    )


def solution(mesh):
    data_count, model_count = mesh.devices.shape
    chips = mesh.devices.reshape(data_count // 8, 4, 2, model_count // 2, 2)
    split = Mesh(chips, DATA + MODEL)
    return jax.shard_map(
        shards,
        mesh=split,
        in_specs=(P(DATA, MODEL), P(DATA, MODEL), P(DATA, MODEL), P(DATA), P(), P()),
        out_specs=P(MODEL, DATA),
        check_vma=False,
    )
```

```python
import math

import jax
import jax.numpy as jnp
from jax import lax
from jax.sharding import Mesh, PartitionSpec as P

D = 8192
HEAD_DIM = 128


EPSILON = 1e-06

CHIPS = ("z", "y_hi")
CORE = "core"
DATA = CHIPS + (CORE,)
MODEL = ("x", "y_lo")


def attend(queries, key_rows, value_rows):
    length = queries.shape[0]
    kv_heads = key_rows.shape[1] // HEAD_DIM
    group_size = queries.shape[1] // HEAD_DIM // kv_heads
    query_four = queries.reshape(length, kv_heads, group_size, HEAD_DIM)
    key_three = key_rows.reshape(length, kv_heads, HEAD_DIM)
    value_three = value_rows.reshape(length, kv_heads, HEAD_DIM)
    scores = jnp.einsum(
        "tkgd,skd->kgts", query_four, key_three, preferred_element_type=jnp.float32
    ) / math.sqrt(HEAD_DIM)
    row_position = lax.broadcasted_iota(jnp.int32, (length, length), 0)
    column_position = lax.broadcasted_iota(jnp.int32, (length, length), 1)
    scores = jnp.where(column_position <= row_position, scores, -jnp.inf)
    weights = jax.nn.softmax(scores, axis=-1).astype(jnp.bfloat16)
    mixture = jnp.einsum(
        "kgts,skd->tkgd", weights, value_three, preferred_element_type=jnp.float32
    )
    return mixture.astype(jnp.bfloat16).reshape(length, queries.shape[1])


def squares_by_row(matrix):
    return jnp.sum(jnp.square(matrix.astype(jnp.float32)), axis=-1)


def inner_rows(left, right):
    return lax.dot_general(
        left, right, (((1,), (1,)), ((), ())), preferred_element_type=jnp.float32
    )


def attend_rows(queries, key_rows, value_rows, rows):
    length = queries.shape[0]
    kv_heads = key_rows.shape[1] // HEAD_DIM
    group_size = queries.shape[1] // HEAD_DIM // kv_heads
    picked = pick_rows(queries, rows)
    query_four = picked.reshape(rows.shape[0], kv_heads, group_size, HEAD_DIM)
    key_three = key_rows.reshape(length, kv_heads, HEAD_DIM)
    value_three = value_rows.reshape(length, kv_heads, HEAD_DIM)
    scores = jnp.einsum(
        "tkgd,skd->kgts", query_four, key_three, preferred_element_type=jnp.float32
    ) / math.sqrt(HEAD_DIM)
    column_position = lax.broadcasted_iota(jnp.int32, (rows.shape[0], length), 1)
    scores = jnp.where(column_position <= rows[:, None], scores, -jnp.inf)
    weights = jax.nn.softmax(scores, axis=-1).astype(jnp.bfloat16)
    mixture = jnp.einsum(
        "kgts,skd->tkgd", weights, value_three, preferred_element_type=jnp.float32
    )
    return mixture.astype(jnp.bfloat16).reshape(rows.shape[0], queries.shape[1])


def pick_rows(matrix, rows):
    hits = rows[:, None] == lax.broadcasted_iota(jnp.int32, (rows.shape[0], matrix.shape[0]), 1)
    return jnp.dot(
        hits.astype(matrix.dtype), matrix, preferred_element_type=jnp.float32
    ).astype(matrix.dtype)


def swap_cores(piece):
    return lax.ppermute(piece, CORE, [(0, 1), (1, 0)])


def gather_marks(query_marks, output_marks):
    data_count = lax.axis_size(DATA)
    kinds = jnp.stack([query_marks, output_marks])
    spread = jnp.broadcast_to(kinds[None], (data_count // 2,) + kinds.shape)
    return lax.all_to_all(
        spread.reshape((data_count,) + query_marks.shape), DATA, 0, 0, tiled=True
    )


def broadcast_gather(piece, axis_name):
    count = lax.axis_size(axis_name)
    spread = jnp.broadcast_to(piece[None], (count,) + piece.shape)
    return lax.all_to_all(spread, axis_name, 0, 0, tiled=True)


def shards(queries, key_rows, value_rows, landmark_index, radius_in, radius_out):
    length = queries.shape[0]
    model_count = lax.axis_size(MODEL)
    data_count = lax.axis_size(DATA)
    model_index = lax.axis_index(MODEL)
    landmarks = radius_in.shape[0]
    row_share = landmarks // model_count
    column_share = landmarks // data_count
    token_count = length * data_count

    own_rows = lax.rem(landmark_index, length)
    first = lax.axis_index(CORE) == 0
    marks = gather_marks(
        pick_rows(queries, own_rows),
        attend_rows(queries, key_rows, value_rows, own_rows),
    ).reshape(landmarks, queries.shape[1])
    attended = attend(queries, key_rows, value_rows)
    own_side = jnp.where(first, queries, attended)
    other_side = swap_cores(jnp.where(first, attended, queries))
    tokens = jnp.stack([own_side, other_side])

    tokens = tokens.reshape(2 * length, queries.shape[1])
    cross = inner_rows(marks, tokens)
    distance_part = (
        squares_by_row(marks)[:, None] + squares_by_row(tokens)[None, :] - 2.0 * cross
    ).reshape(model_count, row_share, 2, length)
    distance = jnp.sum(
        lax.all_to_all(distance_part, MODEL, 0, 0, tiled=True), axis=0
    )
    distance = jnp.transpose(distance, (1, 0, 2))

    radius = jnp.where(first, radius_in, radius_out)
    widths = lax.dynamic_slice_in_dim(radius, model_index * row_share, row_share, 0)
    side = jnp.exp(-distance / (D * widths[None, :, None])).astype(jnp.bfloat16)
    handed = swap_cores(side[1])
    row_features = jnp.where(first, side[0], handed)
    own_columns = jnp.where(first, handed, side[0])
    column_features = broadcast_gather(own_columns, MODEL).reshape(landmarks, length)

    rows32 = row_features.astype(jnp.float32)
    columns32 = column_features.astype(jnp.float32)
    row_mean = jnp.mean(rows32, axis=1)
    column_mean = jnp.mean(columns32, axis=1)
    rows_centered = rows32 - row_mean[:, None]
    columns_centered = columns32 - column_mean[:, None]
    second = lax.dot_general(
        rows_centered,
        columns_centered,
        (((1,), (1,)), ((), ())),
        precision=lax.Precision.HIGH,
        preferred_element_type=jnp.float32,
    )
    row_square = jnp.sum(jnp.square(rows_centered), axis=1)
    column_square = jnp.sum(jnp.square(columns_centered), axis=1)

    packed = jnp.concatenate(
        [
            jnp.transpose(
                second.reshape(row_share, data_count, column_share), (1, 0, 2)
            ).reshape(data_count, row_share * column_share),
            jnp.broadcast_to(row_mean[None], (data_count, row_share)),
            jnp.broadcast_to(row_square[None], (data_count, row_share)),
            column_mean.reshape(data_count, column_share),
            column_square.reshape(data_count, column_share),
        ],
        axis=1,
    )
    received = lax.all_to_all(packed, DATA, 0, 0, tiled=True)
    cut = row_share * column_share
    second_parts = received[:, :cut].reshape(data_count, row_share, column_share)
    row_means = received[:, cut : cut + row_share]
    row_squares = received[:, cut + row_share : cut + 2 * row_share]
    column_means = received[:, cut + 2 * row_share : cut + 2 * row_share + column_share]
    column_squares = received[:, cut + 2 * row_share + column_share :]

    row_shift = row_means - jnp.mean(row_means, axis=0)[None, :]
    column_shift = column_means - jnp.mean(column_means, axis=0)[None, :]
    between = jnp.sum(row_shift[:, :, None] * column_shift[:, None, :], axis=0)
    covariance = (jnp.sum(second_parts, axis=0) + length * between) / token_count
    spread_rows = (
        jnp.sum(row_squares, axis=0) + length * jnp.sum(jnp.square(row_shift), axis=0)
    ) / token_count
    spread_columns = (
        jnp.sum(column_squares, axis=0)
        + length * jnp.sum(jnp.square(column_shift), axis=0)
    ) / token_count
    return covariance / jnp.sqrt(
        (spread_rows + EPSILON)[:, None] * (spread_columns + EPSILON)[None, :]
    )


def solution(mesh):
    data_count, model_count = mesh.devices.shape
    chips = mesh.devices.reshape(data_count // 8, 4, 2, model_count // 2, 2)
    split = Mesh(chips, DATA + MODEL)
    return jax.shard_map(
        shards,
        mesh=split,
        in_specs=(P(DATA, MODEL), P(DATA, MODEL), P(DATA, MODEL), P(DATA), P(), P()),
        out_specs=P(MODEL, DATA),
        check_vma=False,
    )
```

```python
import math

import jax
import jax.numpy as jnp
from jax import lax
from jax.sharding import Mesh, PartitionSpec as P

D = 8192
HEAD_DIM = 128


EPSILON = 1e-06

CHIPS = ("z", "y_hi")
CORE = "core"
DATA = CHIPS + (CORE,)
MODEL = ("x", "y_lo")


def attend(queries, key_rows, value_rows):
    length = queries.shape[0]
    kv_heads = key_rows.shape[1] // HEAD_DIM
    group_size = queries.shape[1] // HEAD_DIM // kv_heads
    query_four = queries.reshape(length, kv_heads, group_size, HEAD_DIM)
    key_three = key_rows.reshape(length, kv_heads, HEAD_DIM)
    value_three = value_rows.reshape(length, kv_heads, HEAD_DIM)
    scores = jnp.einsum(
        "tkgd,skd->kgts", query_four, key_three, preferred_element_type=jnp.float32
    ) / math.sqrt(HEAD_DIM)
    row_position = lax.broadcasted_iota(jnp.int32, (length, length), 0)
    column_position = lax.broadcasted_iota(jnp.int32, (length, length), 1)
    scores = jnp.where(column_position <= row_position, scores, -jnp.inf)
    weights = jax.nn.softmax(scores, axis=-1).astype(jnp.bfloat16)
    mixture = jnp.einsum(
        "kgts,skd->tkgd", weights, value_three, preferred_element_type=jnp.float32
    )
    return mixture.astype(jnp.bfloat16).reshape(length, queries.shape[1])


def squares_by_row(matrix):
    return jnp.sum(jnp.square(matrix.astype(jnp.float32)), axis=-1)


def inner_rows(left, right):
    return lax.dot_general(
        left, right, (((1,), (1,)), ((), ())), preferred_element_type=jnp.float32
    )


def attend_rows(queries, key_rows, value_rows, rows):
    length = queries.shape[0]
    kv_heads = key_rows.shape[1] // HEAD_DIM
    group_size = queries.shape[1] // HEAD_DIM // kv_heads
    picked = pick_rows(queries, rows)
    query_four = picked.reshape(rows.shape[0], kv_heads, group_size, HEAD_DIM)
    key_three = key_rows.reshape(length, kv_heads, HEAD_DIM)
    value_three = value_rows.reshape(length, kv_heads, HEAD_DIM)
    scores = jnp.einsum(
        "tkgd,skd->kgts", query_four, key_three, preferred_element_type=jnp.float32
    ) / math.sqrt(HEAD_DIM)
    column_position = lax.broadcasted_iota(jnp.int32, (rows.shape[0], length), 1)
    scores = jnp.where(column_position <= rows[:, None], scores, -jnp.inf)
    weights = jax.nn.softmax(scores, axis=-1).astype(jnp.bfloat16)
    mixture = jnp.einsum(
        "kgts,skd->tkgd", weights, value_three, preferred_element_type=jnp.float32
    )
    return mixture.astype(jnp.bfloat16).reshape(rows.shape[0], queries.shape[1])


def pick_rows(matrix, rows):
    hits = rows[:, None] == lax.broadcasted_iota(jnp.int32, (rows.shape[0], matrix.shape[0]), 1)
    return jnp.dot(
        hits.astype(matrix.dtype), matrix, preferred_element_type=jnp.float32
    ).astype(matrix.dtype)


def swap_cores(piece):
    return lax.ppermute(piece, CORE, [(0, 1), (1, 0)])


def gather_marks(query_marks, output_marks):
    data_count = lax.axis_size(DATA)
    kinds = jnp.stack([query_marks, output_marks])
    spread = jnp.broadcast_to(kinds[None], (data_count // 2,) + kinds.shape)
    return lax.all_to_all(
        spread.reshape((data_count,) + query_marks.shape), DATA, 0, 0, tiled=True
    )


def broadcast_gather(piece, axis_name):
    count = lax.axis_size(axis_name)
    spread = jnp.broadcast_to(piece[None], (count,) + piece.shape)
    return lax.all_to_all(spread, axis_name, 0, 0, tiled=True)


def shards(queries, key_rows, value_rows, landmark_index, radius_in, radius_out):
    length = queries.shape[0]
    model_count = lax.axis_size(MODEL)
    data_count = lax.axis_size(DATA)
    model_index = lax.axis_index(MODEL)
    landmarks = radius_in.shape[0]
    row_share = landmarks // model_count
    column_share = landmarks // data_count
    token_count = length * data_count

    own_rows = lax.rem(landmark_index, length)
    first = lax.axis_index(CORE) == 0
    marks = gather_marks(
        pick_rows(queries, own_rows),
        attend_rows(queries, key_rows, value_rows, own_rows),
    ).reshape(landmarks, queries.shape[1])
    attended = attend(queries, key_rows, value_rows)
    own_side = jnp.where(first, queries, attended)
    other_side = swap_cores(jnp.where(first, attended, queries))
    tokens = jnp.stack([own_side, other_side])

    tokens = tokens.reshape(2 * length, queries.shape[1])
    cross = inner_rows(marks, tokens)
    distance_part = (
        squares_by_row(marks)[:, None] + squares_by_row(tokens)[None, :] - 2.0 * cross
    ).reshape(model_count, row_share, 2 * length)
    distance = jnp.sum(
        lax.all_to_all(distance_part, MODEL, 0, 0, tiled=True), axis=0
    )

    radius = jnp.where(first, radius_in, radius_out)
    widths = lax.dynamic_slice_in_dim(radius, model_index * row_share, row_share, 0)
    side = jnp.exp(-distance / (D * widths[:, None])).astype(jnp.bfloat16)
    handed = swap_cores(side[:, length:])
    row_features = jnp.where(first, side[:, :length], handed)
    own_columns = jnp.where(first, handed, side[:, :length])
    column_features = broadcast_gather(own_columns, MODEL).reshape(landmarks, length)

    rows32 = row_features.astype(jnp.float32)
    columns32 = column_features.astype(jnp.float32)
    row_mean = jnp.mean(rows32, axis=1)
    column_mean = jnp.mean(columns32, axis=1)
    rows_centered = rows32 - row_mean[:, None]
    columns_centered = columns32 - column_mean[:, None]
    second = lax.dot_general(
        rows_centered,
        columns_centered,
        (((1,), (1,)), ((), ())),
        precision=lax.Precision.HIGH,
        preferred_element_type=jnp.float32,
    )
    row_square = jnp.sum(jnp.square(rows_centered), axis=1)
    column_square = jnp.sum(jnp.square(columns_centered), axis=1)

    packed = jnp.concatenate(
        [
            jnp.transpose(
                second.reshape(row_share, data_count, column_share), (1, 0, 2)
            ).reshape(data_count, row_share * column_share),
            jnp.broadcast_to(row_mean[None], (data_count, row_share)),
            jnp.broadcast_to(row_square[None], (data_count, row_share)),
            column_mean.reshape(data_count, column_share),
            column_square.reshape(data_count, column_share),
        ],
        axis=1,
    )
    received = lax.all_to_all(packed, DATA, 0, 0, tiled=True)
    cut = row_share * column_share
    second_parts = received[:, :cut].reshape(data_count, row_share, column_share)
    row_means = received[:, cut : cut + row_share]
    row_squares = received[:, cut + row_share : cut + 2 * row_share]
    column_means = received[:, cut + 2 * row_share : cut + 2 * row_share + column_share]
    column_squares = received[:, cut + 2 * row_share + column_share :]

    row_shift = row_means - jnp.mean(row_means, axis=0)[None, :]
    column_shift = column_means - jnp.mean(column_means, axis=0)[None, :]
    between = jnp.sum(row_shift[:, :, None] * column_shift[:, None, :], axis=0)
    covariance = (jnp.sum(second_parts, axis=0) + length * between) / token_count
    spread_rows = (
        jnp.sum(row_squares, axis=0) + length * jnp.sum(jnp.square(row_shift), axis=0)
    ) / token_count
    spread_columns = (
        jnp.sum(column_squares, axis=0)
        + length * jnp.sum(jnp.square(column_shift), axis=0)
    ) / token_count
    return covariance / jnp.sqrt(
        (spread_rows + EPSILON)[:, None] * (spread_columns + EPSILON)[None, :]
    )


def solution(mesh):
    data_count, model_count = mesh.devices.shape
    chips = mesh.devices.reshape(data_count // 8, 4, 2, model_count // 2, 2)
    split = Mesh(chips, DATA + MODEL)
    return jax.shard_map(
        shards,
        mesh=split,
        in_specs=(P(DATA, MODEL), P(DATA, MODEL), P(DATA, MODEL), P(DATA), P(), P()),
        out_specs=P(MODEL, DATA),
        check_vma=False,
    )
```

```python
import math

import jax
import jax.numpy as jnp
from jax import lax
from jax.sharding import Mesh, PartitionSpec as P

D = 8192
HEAD_DIM = 128


EPSILON = 1e-06

CHIPS = ("z", "y_hi")
CORE = "core"
DATA = CHIPS + (CORE,)
MODEL = ("x", "y_lo")
PAIR = (CORE,) + MODEL


def attend(queries, key_rows, value_rows):
    length = queries.shape[0]
    kv_heads = key_rows.shape[1] // HEAD_DIM
    group_size = queries.shape[1] // HEAD_DIM // kv_heads
    query_four = queries.reshape(length, kv_heads, group_size, HEAD_DIM)
    key_three = key_rows.reshape(length, kv_heads, HEAD_DIM)
    value_three = value_rows.reshape(length, kv_heads, HEAD_DIM)
    scores = jnp.einsum(
        "tkgd,skd->kgts", query_four, key_three, preferred_element_type=jnp.float32
    ) / math.sqrt(HEAD_DIM)
    row_position = lax.broadcasted_iota(jnp.int32, (length, length), 0)
    column_position = lax.broadcasted_iota(jnp.int32, (length, length), 1)
    scores = jnp.where(column_position <= row_position, scores, -jnp.inf)
    weights = jax.nn.softmax(scores, axis=-1).astype(jnp.bfloat16)
    mixture = jnp.einsum(
        "kgts,skd->tkgd", weights, value_three, preferred_element_type=jnp.float32
    )
    return mixture.astype(jnp.bfloat16).reshape(length, queries.shape[1])


def squares_by_row(matrix):
    return jnp.sum(jnp.square(matrix.astype(jnp.float32)), axis=-1)


def inner_rows(left, right):
    return lax.dot_general(
        left, right, (((1,), (1,)), ((), ())), preferred_element_type=jnp.float32
    )


def attend_rows(queries, key_rows, value_rows, rows):
    length = queries.shape[0]
    kv_heads = key_rows.shape[1] // HEAD_DIM
    group_size = queries.shape[1] // HEAD_DIM // kv_heads
    picked = pick_rows(queries, rows)
    query_four = picked.reshape(rows.shape[0], kv_heads, group_size, HEAD_DIM)
    key_three = key_rows.reshape(length, kv_heads, HEAD_DIM)
    value_three = value_rows.reshape(length, kv_heads, HEAD_DIM)
    scores = jnp.einsum(
        "tkgd,skd->kgts", query_four, key_three, preferred_element_type=jnp.float32
    ) / math.sqrt(HEAD_DIM)
    column_position = lax.broadcasted_iota(jnp.int32, (rows.shape[0], length), 1)
    scores = jnp.where(column_position <= rows[:, None], scores, -jnp.inf)
    weights = jax.nn.softmax(scores, axis=-1).astype(jnp.bfloat16)
    mixture = jnp.einsum(
        "kgts,skd->tkgd", weights, value_three, preferred_element_type=jnp.float32
    )
    return mixture.astype(jnp.bfloat16).reshape(rows.shape[0], queries.shape[1])


def pick_rows(matrix, rows):
    hits = rows[:, None] == lax.broadcasted_iota(jnp.int32, (rows.shape[0], matrix.shape[0]), 1)
    return jnp.dot(
        hits.astype(matrix.dtype), matrix, preferred_element_type=jnp.float32
    ).astype(matrix.dtype)


def swap_cores(piece):
    return lax.ppermute(piece, CORE, [(0, 1), (1, 0)])


def gather_marks(query_marks, output_marks):
    data_count = lax.axis_size(DATA)
    kinds = jnp.stack([query_marks, output_marks])
    spread = jnp.broadcast_to(kinds[None], (data_count // 2,) + kinds.shape)
    return lax.all_to_all(
        spread.reshape((data_count,) + query_marks.shape), DATA, 0, 0, tiled=True
    )


def broadcast_gather(piece, axis_name):
    count = lax.axis_size(axis_name)
    spread = jnp.broadcast_to(piece[None], (count,) + piece.shape)
    return lax.all_to_all(spread, axis_name, 0, 0, tiled=True)


def shards(queries, key_rows, value_rows, landmark_index, radius_in, radius_out):
    length = queries.shape[0]
    model_count = lax.axis_size(MODEL)
    data_count = lax.axis_size(DATA)
    model_index = lax.axis_index(MODEL)
    landmarks = radius_in.shape[0]
    row_share = landmarks // model_count
    column_share = landmarks // data_count
    token_count = length * data_count

    own_rows = lax.rem(landmark_index, length)
    first = lax.axis_index(CORE) == 0
    marks = gather_marks(
        pick_rows(queries, own_rows),
        attend_rows(queries, key_rows, value_rows, own_rows),
    ).reshape(landmarks, queries.shape[1])
    attended = attend(queries, key_rows, value_rows)
    swapped = swap_cores(jnp.where(first, attended, queries))
    tokens = [jnp.where(first, queries, swapped), jnp.where(first, swapped, attended)]

    mark_norms = squares_by_row(marks)
    distance_part = jnp.stack(
        [
            (
                mark_norms[:, None]
                + squares_by_row(rows)[None, :]
                - 2.0 * inner_rows(marks, rows)
            ).reshape(model_count, row_share, length)
            for rows in tokens
        ]
    ).reshape(2 * model_count, row_share, length)
    received = lax.all_to_all(distance_part, PAIR, 0, 0, tiled=True)
    distance = jnp.sum(received.reshape(2, model_count, row_share, length), axis=1)

    widths = lax.dynamic_slice_in_dim(
        jnp.stack([radius_in, radius_out]), model_index * row_share, row_share, 1
    )
    features = jnp.exp(-distance / (D * widths[:, :, None])).astype(jnp.bfloat16)
    row_features = features[0]
    own_columns = features[1]
    column_features = broadcast_gather(own_columns, MODEL).reshape(landmarks, length)

    rows32 = row_features.astype(jnp.float32)
    columns32 = column_features.astype(jnp.float32)
    row_mean = jnp.mean(rows32, axis=1)
    column_mean = jnp.mean(columns32, axis=1)
    rows_centered = rows32 - row_mean[:, None]
    columns_centered = columns32 - column_mean[:, None]
    second = lax.dot_general(
        rows_centered,
        columns_centered,
        (((1,), (1,)), ((), ())),
        precision=lax.Precision.HIGH,
        preferred_element_type=jnp.float32,
    )
    row_square = jnp.sum(jnp.square(rows_centered), axis=1)
    column_square = jnp.sum(jnp.square(columns_centered), axis=1)

    packed = jnp.concatenate(
        [
            jnp.transpose(
                second.reshape(row_share, data_count, column_share), (1, 0, 2)
            ).reshape(data_count, row_share * column_share),
            jnp.broadcast_to(row_mean[None], (data_count, row_share)),
            jnp.broadcast_to(row_square[None], (data_count, row_share)),
            column_mean.reshape(data_count, column_share),
            column_square.reshape(data_count, column_share),
        ],
        axis=1,
    )
    received = lax.all_to_all(packed, DATA, 0, 0, tiled=True)
    cut = row_share * column_share
    second_parts = received[:, :cut].reshape(data_count, row_share, column_share)
    row_means = received[:, cut : cut + row_share]
    row_squares = received[:, cut + row_share : cut + 2 * row_share]
    column_means = received[:, cut + 2 * row_share : cut + 2 * row_share + column_share]
    column_squares = received[:, cut + 2 * row_share + column_share :]

    row_shift = row_means - jnp.mean(row_means, axis=0)[None, :]
    column_shift = column_means - jnp.mean(column_means, axis=0)[None, :]
    between = jnp.sum(row_shift[:, :, None] * column_shift[:, None, :], axis=0)
    covariance = (jnp.sum(second_parts, axis=0) + length * between) / token_count
    spread_rows = (
        jnp.sum(row_squares, axis=0) + length * jnp.sum(jnp.square(row_shift), axis=0)
    ) / token_count
    spread_columns = (
        jnp.sum(column_squares, axis=0)
        + length * jnp.sum(jnp.square(column_shift), axis=0)
    ) / token_count
    return covariance / jnp.sqrt(
        (spread_rows + EPSILON)[:, None] * (spread_columns + EPSILON)[None, :]
    )


def solution(mesh):
    data_count, model_count = mesh.devices.shape
    chips = mesh.devices.reshape(data_count // 8, 4, 2, model_count // 2, 2)
    split = Mesh(chips, DATA + MODEL)
    return jax.shard_map(
        shards,
        mesh=split,
        in_specs=(P(DATA, MODEL), P(DATA, MODEL), P(DATA, MODEL), P(DATA), P(), P()),
        out_specs=P(MODEL, DATA),
        check_vma=False,
    )
```

```python
import math

import jax
import jax.numpy as jnp
from jax import lax
from jax.sharding import Mesh, PartitionSpec as P

D = 8192
HEAD_DIM = 128


EPSILON = 1e-06

CHIPS = ("z", "y_hi")
CORE = "core"
DATA = CHIPS + (CORE,)
MODEL = ("x", "y_lo")
PAIR = (CORE,) + MODEL


def attend(queries, key_rows, value_rows):
    length = queries.shape[0]
    kv_heads = key_rows.shape[1] // HEAD_DIM
    group_size = queries.shape[1] // HEAD_DIM // kv_heads
    query_four = queries.reshape(length, kv_heads, group_size, HEAD_DIM)
    key_three = key_rows.reshape(length, kv_heads, HEAD_DIM)
    value_three = value_rows.reshape(length, kv_heads, HEAD_DIM)
    scores = jnp.einsum(
        "tkgd,skd->kgts", query_four, key_three, preferred_element_type=jnp.float32
    ) / math.sqrt(HEAD_DIM)
    row_position = lax.broadcasted_iota(jnp.int32, (length, length), 0)
    column_position = lax.broadcasted_iota(jnp.int32, (length, length), 1)
    scores = jnp.where(column_position <= row_position, scores, -jnp.inf)
    weights = jax.nn.softmax(scores, axis=-1).astype(jnp.bfloat16)
    mixture = jnp.einsum(
        "kgts,skd->tkgd", weights, value_three, preferred_element_type=jnp.float32
    )
    return mixture.astype(jnp.bfloat16).reshape(length, queries.shape[1])


def squares_by_row(matrix):
    return jnp.sum(jnp.square(matrix.astype(jnp.float32)), axis=-1)


def inner_rows(left, right):
    return lax.dot_general(
        left, right, (((1,), (1,)), ((), ())), preferred_element_type=jnp.float32
    )


def attend_rows(queries, key_rows, value_rows, rows):
    length = queries.shape[0]
    kv_heads = key_rows.shape[1] // HEAD_DIM
    group_size = queries.shape[1] // HEAD_DIM // kv_heads
    picked = pick_rows(queries, rows)
    query_four = picked.reshape(rows.shape[0], kv_heads, group_size, HEAD_DIM)
    key_three = key_rows.reshape(length, kv_heads, HEAD_DIM)
    value_three = value_rows.reshape(length, kv_heads, HEAD_DIM)
    scores = jnp.einsum(
        "tkgd,skd->kgts", query_four, key_three, preferred_element_type=jnp.float32
    ) / math.sqrt(HEAD_DIM)
    column_position = lax.broadcasted_iota(jnp.int32, (rows.shape[0], length), 1)
    scores = jnp.where(column_position <= rows[:, None], scores, -jnp.inf)
    weights = jax.nn.softmax(scores, axis=-1).astype(jnp.bfloat16)
    mixture = jnp.einsum(
        "kgts,skd->tkgd", weights, value_three, preferred_element_type=jnp.float32
    )
    return mixture.astype(jnp.bfloat16).reshape(rows.shape[0], queries.shape[1])


def pick_rows(matrix, rows):
    hits = rows[:, None] == lax.broadcasted_iota(jnp.int32, (rows.shape[0], matrix.shape[0]), 1)
    return jnp.dot(
        hits.astype(matrix.dtype), matrix, preferred_element_type=jnp.float32
    ).astype(matrix.dtype)


def swap_cores(piece):
    return lax.ppermute(piece, CORE, [(0, 1), (1, 0)])


def gather_marks(query_marks, output_marks):
    data_count = lax.axis_size(DATA)
    kinds = jnp.stack([query_marks, output_marks])
    spread = jnp.broadcast_to(kinds[None], (data_count // 2,) + kinds.shape)
    return lax.all_to_all(
        spread.reshape((data_count,) + query_marks.shape), DATA, 0, 0, tiled=True
    )


def broadcast_gather(piece, axis_name):
    count = lax.axis_size(axis_name)
    spread = jnp.broadcast_to(piece[None], (count,) + piece.shape)
    return lax.all_to_all(spread, axis_name, 0, 0, tiled=True)


def shards(queries, key_rows, value_rows, landmark_index, radius_in, radius_out):
    length = queries.shape[0]
    model_count = lax.axis_size(MODEL)
    data_count = lax.axis_size(DATA)
    model_index = lax.axis_index(MODEL)
    landmarks = radius_in.shape[0]
    row_share = landmarks // model_count
    column_share = landmarks // data_count
    token_count = length * data_count

    own_rows = lax.rem(landmark_index, length)
    first = lax.axis_index(CORE) == 0
    marks = gather_marks(
        pick_rows(queries, own_rows),
        attend_rows(queries, key_rows, value_rows, own_rows),
    ).reshape(landmarks, queries.shape[1])
    attended = attend(queries, key_rows, value_rows)
    swapped = swap_cores(jnp.where(first, attended, queries))
    tokens = jnp.stack(
        [jnp.where(first, queries, swapped), jnp.where(first, swapped, attended)]
    )

    cross = jnp.einsum("mc,ktc->kmt", marks, tokens, preferred_element_type=jnp.float32)
    distance_part = (
        squares_by_row(marks)[None, :, None]
        + squares_by_row(tokens)[:, None, :]
        - 2.0 * cross
    ).reshape(2 * model_count, row_share, length)
    received = lax.all_to_all(distance_part, PAIR, 0, 0, tiled=True)
    distance = jnp.sum(received.reshape(2, model_count, row_share, length), axis=1)

    widths = lax.dynamic_slice_in_dim(
        jnp.stack([radius_in, radius_out]), model_index * row_share, row_share, 1
    )
    features = jnp.exp(-distance / (D * widths[:, :, None])).astype(jnp.bfloat16)
    row_features = features[0]
    own_columns = features[1]
    column_features = broadcast_gather(own_columns, MODEL).reshape(landmarks, length)

    rows32 = row_features.astype(jnp.float32)
    columns32 = column_features.astype(jnp.float32)
    row_mean = jnp.mean(rows32, axis=1)
    column_mean = jnp.mean(columns32, axis=1)
    rows_centered = rows32 - row_mean[:, None]
    columns_centered = columns32 - column_mean[:, None]
    second = lax.dot_general(
        rows_centered,
        columns_centered,
        (((1,), (1,)), ((), ())),
        precision=lax.Precision.HIGH,
        preferred_element_type=jnp.float32,
    )
    row_square = jnp.sum(jnp.square(rows_centered), axis=1)
    column_square = jnp.sum(jnp.square(columns_centered), axis=1)

    packed = jnp.concatenate(
        [
            jnp.transpose(
                second.reshape(row_share, data_count, column_share), (1, 0, 2)
            ).reshape(data_count, row_share * column_share),
            jnp.broadcast_to(row_mean[None], (data_count, row_share)),
            jnp.broadcast_to(row_square[None], (data_count, row_share)),
            column_mean.reshape(data_count, column_share),
            column_square.reshape(data_count, column_share),
        ],
        axis=1,
    )
    received = lax.all_to_all(packed, DATA, 0, 0, tiled=True)
    cut = row_share * column_share
    second_parts = received[:, :cut].reshape(data_count, row_share, column_share)
    row_means = received[:, cut : cut + row_share]
    row_squares = received[:, cut + row_share : cut + 2 * row_share]
    column_means = received[:, cut + 2 * row_share : cut + 2 * row_share + column_share]
    column_squares = received[:, cut + 2 * row_share + column_share :]

    row_shift = row_means - jnp.mean(row_means, axis=0)[None, :]
    column_shift = column_means - jnp.mean(column_means, axis=0)[None, :]
    between = jnp.sum(row_shift[:, :, None] * column_shift[:, None, :], axis=0)
    covariance = (jnp.sum(second_parts, axis=0) + length * between) / token_count
    spread_rows = (
        jnp.sum(row_squares, axis=0) + length * jnp.sum(jnp.square(row_shift), axis=0)
    ) / token_count
    spread_columns = (
        jnp.sum(column_squares, axis=0)
        + length * jnp.sum(jnp.square(column_shift), axis=0)
    ) / token_count
    return covariance / jnp.sqrt(
        (spread_rows + EPSILON)[:, None] * (spread_columns + EPSILON)[None, :]
    )


def solution(mesh):
    data_count, model_count = mesh.devices.shape
    chips = mesh.devices.reshape(data_count // 8, 4, 2, model_count // 2, 2)
    split = Mesh(chips, DATA + MODEL)
    return jax.shard_map(
        shards,
        mesh=split,
        in_specs=(P(DATA, MODEL), P(DATA, MODEL), P(DATA, MODEL), P(DATA), P(), P()),
        out_specs=P(MODEL, DATA),
        check_vma=False,
    )
```

```python
import math

import jax
import jax.numpy as jnp
from jax import lax
from jax.sharding import Mesh, PartitionSpec as P

D = 8192
HEAD_DIM = 128


EPSILON = 1e-06

CHIPS = ("z", "y_hi")
CORE = "core"
DATA = CHIPS + (CORE,)
MODEL = ("x", "y_lo")
PAIR = (CORE,) + MODEL


def attend(queries, key_rows, value_rows):
    length = queries.shape[0]
    kv_heads = key_rows.shape[1] // HEAD_DIM
    group_size = queries.shape[1] // HEAD_DIM // kv_heads
    query_four = queries.reshape(length, kv_heads, group_size, HEAD_DIM)
    key_three = key_rows.reshape(length, kv_heads, HEAD_DIM)
    value_three = value_rows.reshape(length, kv_heads, HEAD_DIM)
    scores = jnp.einsum(
        "tkgd,skd->kgts", query_four, key_three, preferred_element_type=jnp.float32
    ) / math.sqrt(HEAD_DIM)
    row_position = lax.broadcasted_iota(jnp.int32, (length, length), 0)
    column_position = lax.broadcasted_iota(jnp.int32, (length, length), 1)
    scores = jnp.where(column_position <= row_position, scores, -jnp.inf)
    weights = jax.nn.softmax(scores, axis=-1).astype(jnp.bfloat16)
    mixture = jnp.einsum(
        "kgts,skd->tkgd", weights, value_three, preferred_element_type=jnp.float32
    )
    return mixture.astype(jnp.bfloat16).reshape(length, queries.shape[1])


def squares_by_row(matrix):
    return jnp.sum(jnp.square(matrix.astype(jnp.float32)), axis=-1)


def inner_rows(left, right):
    return lax.dot_general(
        left, right, (((1,), (1,)), ((), ())), preferred_element_type=jnp.float32
    )


def attend_rows(queries, key_rows, value_rows, rows):
    length = queries.shape[0]
    kv_heads = key_rows.shape[1] // HEAD_DIM
    group_size = queries.shape[1] // HEAD_DIM // kv_heads
    picked = pick_rows(queries, rows)
    query_four = picked.reshape(rows.shape[0], kv_heads, group_size, HEAD_DIM)
    key_three = key_rows.reshape(length, kv_heads, HEAD_DIM)
    value_three = value_rows.reshape(length, kv_heads, HEAD_DIM)
    scores = jnp.einsum(
        "tkgd,skd->kgts", query_four, key_three, preferred_element_type=jnp.float32
    ) / math.sqrt(HEAD_DIM)
    column_position = lax.broadcasted_iota(jnp.int32, (rows.shape[0], length), 1)
    scores = jnp.where(column_position <= rows[:, None], scores, -jnp.inf)
    weights = jax.nn.softmax(scores, axis=-1).astype(jnp.bfloat16)
    mixture = jnp.einsum(
        "kgts,skd->tkgd", weights, value_three, preferred_element_type=jnp.float32
    )
    return mixture.astype(jnp.bfloat16).reshape(rows.shape[0], queries.shape[1])


def pick_rows(matrix, rows):
    return jnp.concatenate(
        [lax.dynamic_slice_in_dim(matrix, rows[i], 1, 0) for i in range(rows.shape[0])]
    )


def swap_cores(piece):
    return lax.ppermute(piece, CORE, [(0, 1), (1, 0)])


def gather_marks(query_marks, output_marks):
    data_count = lax.axis_size(DATA)
    kinds = jnp.stack([query_marks, output_marks])
    spread = jnp.broadcast_to(kinds[None], (data_count // 2,) + kinds.shape)
    return lax.all_to_all(
        spread.reshape((data_count,) + query_marks.shape), DATA, 0, 0, tiled=True
    )


def broadcast_gather(piece, axis_name):
    count = lax.axis_size(axis_name)
    spread = jnp.broadcast_to(piece[None], (count,) + piece.shape)
    return lax.all_to_all(spread, axis_name, 0, 0, tiled=True)


def shards(queries, key_rows, value_rows, landmark_index, radius_in, radius_out):
    length = queries.shape[0]
    model_count = lax.axis_size(MODEL)
    data_count = lax.axis_size(DATA)
    model_index = lax.axis_index(MODEL)
    landmarks = radius_in.shape[0]
    row_share = landmarks // model_count
    column_share = landmarks // data_count
    token_count = length * data_count

    own_rows = lax.rem(landmark_index, length)
    first = lax.axis_index(CORE) == 0
    marks = gather_marks(
        pick_rows(queries, own_rows),
        attend_rows(queries, key_rows, value_rows, own_rows),
    ).reshape(landmarks, queries.shape[1])
    attended = attend(queries, key_rows, value_rows)
    swapped = swap_cores(jnp.where(first, attended, queries))
    tokens = [jnp.where(first, queries, swapped), jnp.where(first, swapped, attended)]

    mark_norms = squares_by_row(marks)
    distance_part = jnp.stack(
        [
            (
                mark_norms[:, None]
                + squares_by_row(rows)[None, :]
                - 2.0 * inner_rows(marks, rows)
            ).reshape(model_count, row_share, length)
            for rows in tokens
        ]
    ).reshape(2 * model_count, row_share, length)
    received = lax.all_to_all(distance_part, PAIR, 0, 0, tiled=True)
    distance = jnp.sum(received.reshape(2, model_count, row_share, length), axis=1)

    widths = lax.dynamic_slice_in_dim(
        jnp.stack([radius_in, radius_out]), model_index * row_share, row_share, 1
    )
    features = jnp.exp(-distance / (D * widths[:, :, None])).astype(jnp.bfloat16)
    row_features = features[0]
    own_columns = features[1]
    column_features = broadcast_gather(own_columns, MODEL).reshape(landmarks, length)

    rows32 = row_features.astype(jnp.float32)
    columns32 = column_features.astype(jnp.float32)
    row_mean = jnp.mean(rows32, axis=1)
    column_mean = jnp.mean(columns32, axis=1)
    rows_centered = rows32 - row_mean[:, None]
    columns_centered = columns32 - column_mean[:, None]
    second = lax.dot_general(
        rows_centered,
        columns_centered,
        (((1,), (1,)), ((), ())),
        precision=lax.Precision.HIGH,
        preferred_element_type=jnp.float32,
    )
    row_square = jnp.sum(jnp.square(rows_centered), axis=1)
    column_square = jnp.sum(jnp.square(columns_centered), axis=1)

    packed = jnp.concatenate(
        [
            jnp.transpose(
                second.reshape(row_share, data_count, column_share), (1, 0, 2)
            ).reshape(data_count, row_share * column_share),
            jnp.broadcast_to(row_mean[None], (data_count, row_share)),
            jnp.broadcast_to(row_square[None], (data_count, row_share)),
            column_mean.reshape(data_count, column_share),
            column_square.reshape(data_count, column_share),
        ],
        axis=1,
    )
    received = lax.all_to_all(packed, DATA, 0, 0, tiled=True)
    cut = row_share * column_share
    second_parts = received[:, :cut].reshape(data_count, row_share, column_share)
    row_means = received[:, cut : cut + row_share]
    row_squares = received[:, cut + row_share : cut + 2 * row_share]
    column_means = received[:, cut + 2 * row_share : cut + 2 * row_share + column_share]
    column_squares = received[:, cut + 2 * row_share + column_share :]

    row_shift = row_means - jnp.mean(row_means, axis=0)[None, :]
    column_shift = column_means - jnp.mean(column_means, axis=0)[None, :]
    between = jnp.sum(row_shift[:, :, None] * column_shift[:, None, :], axis=0)
    covariance = (jnp.sum(second_parts, axis=0) + length * between) / token_count
    spread_rows = (
        jnp.sum(row_squares, axis=0) + length * jnp.sum(jnp.square(row_shift), axis=0)
    ) / token_count
    spread_columns = (
        jnp.sum(column_squares, axis=0)
        + length * jnp.sum(jnp.square(column_shift), axis=0)
    ) / token_count
    return covariance / jnp.sqrt(
        (spread_rows + EPSILON)[:, None] * (spread_columns + EPSILON)[None, :]
    )


def solution(mesh):
    data_count, model_count = mesh.devices.shape
    chips = mesh.devices.reshape(data_count // 8, 4, 2, model_count // 2, 2)
    split = Mesh(chips, DATA + MODEL)
    return jax.shard_map(
        shards,
        mesh=split,
        in_specs=(P(DATA, MODEL), P(DATA, MODEL), P(DATA, MODEL), P(DATA), P(), P()),
        out_specs=P(MODEL, DATA),
        check_vma=False,
    )
```

```python
import math

import jax
import jax.numpy as jnp
from jax import lax
from jax.sharding import Mesh, PartitionSpec as P

D = 8192
HEAD_DIM = 128


EPSILON = 1e-06

CHIPS = ("z", "y_hi")
CORE = "core"
DATA = CHIPS + (CORE,)
MODEL = ("x", "y_lo")
PAIR = (CORE,) + MODEL


def attend(queries, key_rows, value_rows):
    length = queries.shape[0]
    kv_heads = key_rows.shape[1] // HEAD_DIM
    group_size = queries.shape[1] // HEAD_DIM // kv_heads
    query_four = queries.reshape(length, kv_heads, group_size, HEAD_DIM)
    key_three = key_rows.reshape(length, kv_heads, HEAD_DIM)
    value_three = value_rows.reshape(length, kv_heads, HEAD_DIM)
    scores = jnp.einsum(
        "tkgd,skd->kgts", query_four, key_three, preferred_element_type=jnp.float32
    ) / math.sqrt(HEAD_DIM)
    row_position = lax.broadcasted_iota(jnp.int32, (length, length), 0)
    column_position = lax.broadcasted_iota(jnp.int32, (length, length), 1)
    scores = jnp.where(column_position <= row_position, scores, -jnp.inf)
    weights = jax.nn.softmax(scores, axis=-1).astype(jnp.bfloat16)
    mixture = jnp.einsum(
        "kgts,skd->tkgd", weights, value_three, preferred_element_type=jnp.float32
    )
    return mixture.astype(jnp.bfloat16).reshape(length, queries.shape[1])


def squares_by_row(matrix):
    return jnp.sum(jnp.square(matrix.astype(jnp.float32)), axis=-1)


def inner_rows(left, right):
    return lax.dot_general(
        left, right, (((1,), (1,)), ((), ())), preferred_element_type=jnp.float32
    )


def attend_rows(queries, key_rows, value_rows, rows):
    length = queries.shape[0]
    kv_heads = key_rows.shape[1] // HEAD_DIM
    group_size = queries.shape[1] // HEAD_DIM // kv_heads
    picked = pick_rows(queries, rows)
    query_four = picked.reshape(rows.shape[0], kv_heads, group_size, HEAD_DIM)
    key_three = key_rows.reshape(length, kv_heads, HEAD_DIM)
    value_three = value_rows.reshape(length, kv_heads, HEAD_DIM)
    scores = jnp.einsum(
        "tkgd,skd->kgts", query_four, key_three, preferred_element_type=jnp.float32
    ) / math.sqrt(HEAD_DIM)
    column_position = lax.broadcasted_iota(jnp.int32, (rows.shape[0], length), 1)
    scores = jnp.where(column_position <= rows[:, None], scores, -jnp.inf)
    weights = jax.nn.softmax(scores, axis=-1).astype(jnp.bfloat16)
    mixture = jnp.einsum(
        "kgts,skd->tkgd", weights, value_three, preferred_element_type=jnp.float32
    )
    return mixture.astype(jnp.bfloat16).reshape(rows.shape[0], queries.shape[1])


def pick_rows(matrix, rows):
    hits = rows[:, None] == lax.broadcasted_iota(jnp.int32, (rows.shape[0], matrix.shape[0]), 1)
    return jnp.dot(
        hits.astype(matrix.dtype), matrix, preferred_element_type=jnp.float32
    ).astype(matrix.dtype)


def swap_cores(piece):
    return lax.ppermute(piece, CORE, [(0, 1), (1, 0)])


def gather_marks(query_marks, output_marks):
    data_count = lax.axis_size(DATA)
    kinds = jnp.stack([query_marks, output_marks])
    spread = jnp.broadcast_to(kinds[None], (data_count // 2,) + kinds.shape)
    return lax.all_to_all(
        spread.reshape((data_count,) + query_marks.shape), DATA, 0, 0, tiled=True
    )


def broadcast_gather(piece, axis_name):
    count = lax.axis_size(axis_name)
    spread = jnp.broadcast_to(piece[None], (count,) + piece.shape)
    return lax.all_to_all(spread, axis_name, 0, 0, tiled=True)


def shards(queries, key_rows, value_rows, landmark_index, radius_in, radius_out):
    length = queries.shape[0]
    model_count = lax.axis_size(MODEL)
    data_count = lax.axis_size(DATA)
    model_index = lax.axis_index(MODEL)
    landmarks = radius_in.shape[0]
    row_share = landmarks // model_count
    column_share = landmarks // data_count
    token_count = length * data_count

    own_rows = lax.rem(landmark_index, length)
    first = lax.axis_index(CORE) == 0
    marks = gather_marks(
        pick_rows(queries, own_rows),
        attend_rows(queries, key_rows, value_rows, own_rows),
    ).reshape(landmarks, queries.shape[1])
    attended = attend(queries, key_rows, value_rows)
    swapped = swap_cores(jnp.where(first, attended, queries))
    tokens = [jnp.where(first, queries, swapped), jnp.where(first, swapped, attended)]

    mark_norms = squares_by_row(marks)
    distance_part = jnp.stack(
        [
            (
                mark_norms[:, None]
                + squares_by_row(rows)[None, :]
                - 2.0 * inner_rows(marks, rows)
            ).reshape(model_count, row_share, length)
            for rows in tokens
        ]
    ).reshape(2 * model_count, row_share, length)
    received = lax.all_to_all(distance_part, PAIR, 0, 0, tiled=True)
    distance = jnp.sum(received.reshape(2, model_count, row_share, length), axis=1)

    widths = lax.dynamic_slice_in_dim(
        jnp.stack([radius_in, radius_out]), model_index * row_share, row_share, 1
    )
    features = jnp.exp(-distance / (D * widths[:, :, None])).astype(jnp.bfloat16)
    row_features = features[0]
    own_columns = features[1]
    column_features = broadcast_gather(own_columns, MODEL).reshape(landmarks, length)

    rows32 = row_features.astype(jnp.float32)
    columns32 = column_features.astype(jnp.float32)
    row_mean = jnp.mean(rows32, axis=1)
    column_mean = jnp.mean(columns32, axis=1)
    rows_centered = rows32 - row_mean[:, None]
    columns_centered = columns32 - column_mean[:, None]
    second = lax.dot_general(
        rows_centered,
        columns_centered,
        (((1,), (1,)), ((), ())),
        precision=lax.Precision.HIGH,
        preferred_element_type=jnp.float32,
    )
    row_square = jnp.sum(jnp.square(rows_centered), axis=1)
    column_square = jnp.sum(jnp.square(columns_centered), axis=1)

    packed = jnp.concatenate(
        [
            jnp.transpose(
                second.reshape(row_share, data_count, column_share), (1, 0, 2)
            ).reshape(data_count, row_share * column_share),
            jnp.broadcast_to(row_mean[None], (data_count, row_share)),
            jnp.broadcast_to(row_square[None], (data_count, row_share)),
            column_mean.reshape(data_count, column_share),
            column_square.reshape(data_count, column_share),
        ],
        axis=1,
    )
    width = packed.shape[1]
    padded = jnp.pad(packed, ((0, 0), (0, -width % 1024))).reshape(data_count, -1, 8, 128)
    received = lax.all_to_all(padded, DATA, 0, 0, tiled=True)
    received = received.reshape(data_count, -1)[:, :width]
    cut = row_share * column_share
    second_parts = received[:, :cut].reshape(data_count, row_share, column_share)
    row_means = received[:, cut : cut + row_share]
    row_squares = received[:, cut + row_share : cut + 2 * row_share]
    column_means = received[:, cut + 2 * row_share : cut + 2 * row_share + column_share]
    column_squares = received[:, cut + 2 * row_share + column_share :]

    row_shift = row_means - jnp.mean(row_means, axis=0)[None, :]
    column_shift = column_means - jnp.mean(column_means, axis=0)[None, :]
    between = jnp.sum(row_shift[:, :, None] * column_shift[:, None, :], axis=0)
    covariance = (jnp.sum(second_parts, axis=0) + length * between) / token_count
    spread_rows = (
        jnp.sum(row_squares, axis=0) + length * jnp.sum(jnp.square(row_shift), axis=0)
    ) / token_count
    spread_columns = (
        jnp.sum(column_squares, axis=0)
        + length * jnp.sum(jnp.square(column_shift), axis=0)
    ) / token_count
    return covariance / jnp.sqrt(
        (spread_rows + EPSILON)[:, None] * (spread_columns + EPSILON)[None, :]
    )


def solution(mesh):
    data_count, model_count = mesh.devices.shape
    chips = mesh.devices.reshape(data_count // 8, 4, 2, model_count // 2, 2)
    split = Mesh(chips, DATA + MODEL)
    return jax.shard_map(
        shards,
        mesh=split,
        in_specs=(P(DATA, MODEL), P(DATA, MODEL), P(DATA, MODEL), P(DATA), P(), P()),
        out_specs=P(MODEL, DATA),
        check_vma=False,
    )
```

```python
import math

import jax
import jax.numpy as jnp
from jax import lax
from jax.sharding import Mesh, PartitionSpec as P

D = 8192
HEAD_DIM = 128


EPSILON = 1e-06

CHIPS = ("z", "y_hi")
CORE = "core"
DATA = CHIPS + (CORE,)
MODEL = ("x", "y_lo")
PAIR = (CORE,) + MODEL


def attend(queries, key_rows, value_rows):
    length = queries.shape[0]
    kv_heads = key_rows.shape[1] // HEAD_DIM
    group_size = queries.shape[1] // HEAD_DIM // kv_heads
    query_four = queries.reshape(length, kv_heads, group_size, HEAD_DIM)
    key_three = key_rows.reshape(length, kv_heads, HEAD_DIM)
    value_three = value_rows.reshape(length, kv_heads, HEAD_DIM)
    scores = jnp.einsum(
        "tkgd,skd->kgts", query_four, key_three, preferred_element_type=jnp.float32
    ) / math.sqrt(HEAD_DIM)
    row_position = lax.broadcasted_iota(jnp.int32, (length, length), 0)
    column_position = lax.broadcasted_iota(jnp.int32, (length, length), 1)
    scores = jnp.where(column_position <= row_position, scores, -jnp.inf)
    weights = jax.nn.softmax(scores, axis=-1).astype(jnp.bfloat16)
    mixture = jnp.einsum(
        "kgts,skd->tkgd", weights, value_three, preferred_element_type=jnp.float32
    )
    return mixture.astype(jnp.bfloat16).reshape(length, queries.shape[1])


def squares_by_row(matrix):
    return jnp.sum(jnp.square(matrix.astype(jnp.float32)), axis=-1)


def inner_rows(left, right):
    return lax.dot_general(
        left, right, (((1,), (1,)), ((), ())), preferred_element_type=jnp.float32
    )


def attend_rows(queries, key_rows, value_rows, rows, start):
    length = queries.shape[0]
    kv_heads = key_rows.shape[1] // HEAD_DIM
    group_size = queries.shape[1] // HEAD_DIM // kv_heads
    picked = pick_rows(queries, rows, start)
    query_four = picked.reshape(rows.shape[0], kv_heads, group_size, HEAD_DIM)
    key_three = key_rows.reshape(length, kv_heads, HEAD_DIM)
    value_three = value_rows.reshape(length, kv_heads, HEAD_DIM)
    scores = jnp.einsum(
        "tkgd,skd->kgts", query_four, key_three, preferred_element_type=jnp.float32
    ) / math.sqrt(HEAD_DIM)
    column_position = lax.broadcasted_iota(jnp.int32, (rows.shape[0], length), 1)
    scores = jnp.where(column_position + start <= rows[:, None], scores, -jnp.inf)
    weights = jax.nn.softmax(scores, axis=-1).astype(jnp.bfloat16)
    mixture = jnp.einsum(
        "kgts,skd->tkgd", weights, value_three, preferred_element_type=jnp.float32
    )
    return mixture.astype(jnp.bfloat16).reshape(rows.shape[0], queries.shape[1])


def pick_rows(matrix, rows, start):
    hits = rows[:, None] == start + lax.broadcasted_iota(jnp.int32, (rows.shape[0], matrix.shape[0]), 1)
    return jnp.dot(
        hits.astype(matrix.dtype), matrix, preferred_element_type=jnp.float32
    ).astype(matrix.dtype)


def swap_cores(piece):
    return lax.ppermute(piece, CORE, [(0, 1), (1, 0)])


def gather_marks(query_marks, output_marks):
    data_count = lax.axis_size(DATA)
    kinds = jnp.stack([query_marks, output_marks])
    spread = jnp.broadcast_to(kinds[None], (data_count // 2,) + kinds.shape)
    return lax.all_to_all(
        spread.reshape((data_count,) + query_marks.shape), DATA, 0, 0, tiled=True
    )


def broadcast_gather(piece, axis_name):
    count = lax.axis_size(axis_name)
    spread = jnp.broadcast_to(piece[None], (count,) + piece.shape)
    return lax.all_to_all(spread, axis_name, 0, 0, tiled=True)


def shards(queries, key_rows, value_rows, landmark_index, radius_in, radius_out):
    length = queries.shape[0]
    model_count = lax.axis_size(MODEL)
    data_count = lax.axis_size(DATA)
    model_index = lax.axis_index(MODEL)
    landmarks = radius_in.shape[0]
    row_share = landmarks // model_count
    column_share = landmarks // data_count
    token_count = length * data_count

    start = lax.axis_index(DATA) * length
    first = lax.axis_index(CORE) == 0
    marks = gather_marks(
        pick_rows(queries, landmark_index, start),
        attend_rows(queries, key_rows, value_rows, landmark_index, start),
    ).reshape(landmarks, queries.shape[1])
    attended = attend(queries, key_rows, value_rows)
    swapped = swap_cores(jnp.where(first, attended, queries))
    tokens = [jnp.where(first, queries, swapped), jnp.where(first, swapped, attended)]

    mark_norms = squares_by_row(marks)
    distance_part = jnp.stack(
        [
            (
                mark_norms[:, None]
                + squares_by_row(rows)[None, :]
                - 2.0 * inner_rows(marks, rows)
            ).reshape(model_count, row_share, length)
            for rows in tokens
        ]
    ).reshape(2 * model_count, row_share, length)
    received = lax.all_to_all(distance_part, PAIR, 0, 0, tiled=True)
    distance = jnp.sum(received.reshape(2, model_count, row_share, length), axis=1)

    widths = lax.dynamic_slice_in_dim(
        jnp.stack([radius_in, radius_out]), model_index * row_share, row_share, 1
    )
    features = jnp.exp(-distance / (D * widths[:, :, None])).astype(jnp.bfloat16)
    row_features = features[0]
    own_columns = features[1]
    column_features = broadcast_gather(own_columns, MODEL).reshape(landmarks, length)

    rows32 = row_features.astype(jnp.float32)
    columns32 = column_features.astype(jnp.float32)
    row_mean = jnp.mean(rows32, axis=1)
    column_mean = jnp.mean(columns32, axis=1)
    rows_centered = rows32 - row_mean[:, None]
    columns_centered = columns32 - column_mean[:, None]
    second = lax.dot_general(
        rows_centered,
        columns_centered,
        (((1,), (1,)), ((), ())),
        precision=lax.Precision.HIGH,
        preferred_element_type=jnp.float32,
    )
    row_square = jnp.sum(jnp.square(rows_centered), axis=1)
    column_square = jnp.sum(jnp.square(columns_centered), axis=1)

    packed = jnp.concatenate(
        [
            jnp.transpose(
                second.reshape(row_share, data_count, column_share), (1, 0, 2)
            ).reshape(data_count, row_share * column_share),
            jnp.broadcast_to(row_mean[None], (data_count, row_share)),
            jnp.broadcast_to(row_square[None], (data_count, row_share)),
            column_mean.reshape(data_count, column_share),
            column_square.reshape(data_count, column_share),
        ],
        axis=1,
    )
    received = lax.all_to_all(packed, DATA, 0, 0, tiled=True)
    cut = row_share * column_share
    second_parts = received[:, :cut].reshape(data_count, row_share, column_share)
    row_means = received[:, cut : cut + row_share]
    row_squares = received[:, cut + row_share : cut + 2 * row_share]
    column_means = received[:, cut + 2 * row_share : cut + 2 * row_share + column_share]
    column_squares = received[:, cut + 2 * row_share + column_share :]

    row_shift = row_means - jnp.mean(row_means, axis=0)[None, :]
    column_shift = column_means - jnp.mean(column_means, axis=0)[None, :]
    between = jnp.sum(row_shift[:, :, None] * column_shift[:, None, :], axis=0)
    covariance = (jnp.sum(second_parts, axis=0) + length * between) / token_count
    spread_rows = (
        jnp.sum(row_squares, axis=0) + length * jnp.sum(jnp.square(row_shift), axis=0)
    ) / token_count
    spread_columns = (
        jnp.sum(column_squares, axis=0)
        + length * jnp.sum(jnp.square(column_shift), axis=0)
    ) / token_count
    return covariance / jnp.sqrt(
        (spread_rows + EPSILON)[:, None] * (spread_columns + EPSILON)[None, :]
    )


def solution(mesh):
    data_count, model_count = mesh.devices.shape
    chips = mesh.devices.reshape(data_count // 8, 4, 2, model_count // 2, 2)
    split = Mesh(chips, DATA + MODEL)
    return jax.shard_map(
        shards,
        mesh=split,
        in_specs=(P(DATA, MODEL), P(DATA, MODEL), P(DATA, MODEL), P(DATA), P(), P()),
        out_specs=P(MODEL, DATA),
        check_vma=False,
    )
```

```python
import math

import jax
import jax.numpy as jnp
from jax import lax
from jax.sharding import Mesh, PartitionSpec as P

D = 8192
HEAD_DIM = 128


EPSILON = 1e-06

CHIPS = ("z", "y_hi")
CORE = "core"
DATA = CHIPS + (CORE,)
MODEL = ("x", "y_lo")
PAIR = (CORE,) + MODEL


def attend(queries, key_rows, value_rows):
    length = queries.shape[0]
    kv_heads = key_rows.shape[1] // HEAD_DIM
    group_size = queries.shape[1] // HEAD_DIM // kv_heads
    query_four = queries.reshape(length, kv_heads, group_size, HEAD_DIM)
    key_three = key_rows.reshape(length, kv_heads, HEAD_DIM)
    value_three = value_rows.reshape(length, kv_heads, HEAD_DIM)
    scores = jnp.einsum(
        "tkgd,skd->kgts", query_four, key_three, preferred_element_type=jnp.float32
    ) / math.sqrt(HEAD_DIM)
    row_position = lax.broadcasted_iota(jnp.int32, (length, length), 0)
    column_position = lax.broadcasted_iota(jnp.int32, (length, length), 1)
    scores = jnp.where(column_position <= row_position, scores, -jnp.inf)
    weights = jax.nn.softmax(scores, axis=-1).astype(jnp.bfloat16)
    mixture = jnp.einsum(
        "kgts,skd->tkgd", weights, value_three, preferred_element_type=jnp.float32
    )
    return mixture.astype(jnp.bfloat16).reshape(length, queries.shape[1])


def squares_by_row(matrix):
    return jnp.sum(jnp.square(matrix.astype(jnp.float32)), axis=-1)


def inner_rows(left, right):
    return lax.dot_general(
        left, right, (((1,), (1,)), ((), ())), preferred_element_type=jnp.float32
    )


def attend_rows(queries, key_rows, value_rows, rows):
    length = queries.shape[0]
    kv_heads = key_rows.shape[1] // HEAD_DIM
    group_size = queries.shape[1] // HEAD_DIM // kv_heads
    picked = pick_rows(queries, rows)
    query_four = picked.reshape(rows.shape[0], kv_heads, group_size, HEAD_DIM)
    key_three = key_rows.reshape(length, kv_heads, HEAD_DIM)
    value_three = value_rows.reshape(length, kv_heads, HEAD_DIM)
    scores = jnp.einsum(
        "tkgd,skd->kgts", query_four, key_three, preferred_element_type=jnp.float32
    ) / math.sqrt(HEAD_DIM)
    column_position = lax.broadcasted_iota(jnp.int32, (rows.shape[0], length), 1)
    scores = jnp.where(column_position <= rows[:, None], scores, -jnp.inf)
    weights = jax.nn.softmax(scores, axis=-1).astype(jnp.bfloat16)
    mixture = jnp.einsum(
        "kgts,skd->tkgd", weights, value_three, preferred_element_type=jnp.float32
    )
    return mixture.astype(jnp.bfloat16).reshape(rows.shape[0], queries.shape[1])


def pick_rows(matrix, rows):
    hits = rows[:, None] == lax.broadcasted_iota(jnp.int32, (rows.shape[0], matrix.shape[0]), 1)
    return jnp.dot(
        hits.astype(matrix.dtype), matrix, preferred_element_type=jnp.float32
    ).astype(matrix.dtype)


def swap_cores(piece):
    return lax.ppermute(piece, CORE, [(0, 1), (1, 0)])


def gather_marks(query_marks, output_marks):
    data_count = lax.axis_size(DATA)
    kinds = jnp.stack([query_marks, output_marks])
    spread = jnp.broadcast_to(kinds[None], (data_count // 2,) + kinds.shape)
    return lax.all_to_all(
        spread.reshape((data_count,) + query_marks.shape), DATA, 0, 0, tiled=True
    )


def broadcast_gather(piece, axis_name):
    count = lax.axis_size(axis_name)
    spread = jnp.broadcast_to(piece[None], (count,) + piece.shape)
    return lax.all_to_all(spread, axis_name, 0, 0, tiled=True)


def shards(queries, key_rows, value_rows, landmark_index, radius_in, radius_out):
    length = queries.shape[0]
    model_count = lax.axis_size(MODEL)
    data_count = lax.axis_size(DATA)
    model_index = lax.axis_index(MODEL)
    landmarks = radius_in.shape[0]
    row_share = landmarks // model_count
    column_share = landmarks // data_count
    token_count = length * data_count

    own_rows = lax.rem(landmark_index, length)
    first = lax.axis_index(CORE) == 0
    marks = gather_marks(
        pick_rows(queries, own_rows),
        attend_rows(queries, key_rows, value_rows, own_rows),
    ).reshape(landmarks, queries.shape[1])
    attended = attend(queries, key_rows, value_rows)
    swapped = swap_cores(jnp.where(first, attended, queries))
    tokens = [jnp.where(first, queries, swapped), jnp.where(first, swapped, attended)]

    mark_norms = squares_by_row(marks)
    distance_part = jnp.stack(
        [
            (
                mark_norms[:, None]
                + squares_by_row(rows)[None, :]
                - 2.0 * inner_rows(marks, rows)
            ).reshape(model_count, row_share, length)
            for rows in tokens
        ]
    ).reshape(2 * model_count, row_share, length)
    received = lax.all_to_all(distance_part, PAIR, 0, 0, tiled=True)
    distance = jnp.sum(received.reshape(2, model_count, row_share, length), axis=1)

    widths = lax.dynamic_slice_in_dim(
        jnp.stack([radius_in, radius_out]), model_index * row_share, row_share, 1
    )
    features = jnp.exp(-distance / (D * widths[:, :, None])).astype(jnp.bfloat16)
    row_features = features[0]
    own_columns = features[1]
    column_features = broadcast_gather(own_columns, MODEL).reshape(landmarks, length)

    rows32 = row_features.astype(jnp.float32)
    columns32 = column_features.astype(jnp.float32)
    row_mean = jnp.mean(rows32, axis=1)
    column_mean = jnp.mean(columns32, axis=1)
    rows_centered = (rows32 - row_mean[:, None]).astype(jnp.bfloat16)
    columns_centered = (columns32 - column_mean[:, None]).astype(jnp.bfloat16)
    second = lax.dot_general(
        rows_centered,
        columns_centered,
        (((1,), (1,)), ((), ())),
        preferred_element_type=jnp.float32,
    )
    row_square = jnp.sum(jnp.square(rows_centered.astype(jnp.float32)), axis=1)
    column_square = jnp.sum(jnp.square(columns_centered.astype(jnp.float32)), axis=1)

    packed = jnp.concatenate(
        [
            jnp.transpose(
                second.reshape(row_share, data_count, column_share), (1, 0, 2)
            ).reshape(data_count, row_share * column_share),
            jnp.broadcast_to(row_mean[None], (data_count, row_share)),
            jnp.broadcast_to(row_square[None], (data_count, row_share)),
            column_mean.reshape(data_count, column_share),
            column_square.reshape(data_count, column_share),
        ],
        axis=1,
    )
    received = lax.all_to_all(packed, DATA, 0, 0, tiled=True)
    cut = row_share * column_share
    second_parts = received[:, :cut].reshape(data_count, row_share, column_share)
    row_means = received[:, cut : cut + row_share]
    row_squares = received[:, cut + row_share : cut + 2 * row_share]
    column_means = received[:, cut + 2 * row_share : cut + 2 * row_share + column_share]
    column_squares = received[:, cut + 2 * row_share + column_share :]

    row_shift = row_means - jnp.mean(row_means, axis=0)[None, :]
    column_shift = column_means - jnp.mean(column_means, axis=0)[None, :]
    between = jnp.sum(row_shift[:, :, None] * column_shift[:, None, :], axis=0)
    covariance = (jnp.sum(second_parts, axis=0) + length * between) / token_count
    spread_rows = (
        jnp.sum(row_squares, axis=0) + length * jnp.sum(jnp.square(row_shift), axis=0)
    ) / token_count
    spread_columns = (
        jnp.sum(column_squares, axis=0)
        + length * jnp.sum(jnp.square(column_shift), axis=0)
    ) / token_count
    return covariance / jnp.sqrt(
        (spread_rows + EPSILON)[:, None] * (spread_columns + EPSILON)[None, :]
    )


def solution(mesh):
    data_count, model_count = mesh.devices.shape
    chips = mesh.devices.reshape(data_count // 8, 4, 2, model_count // 2, 2)
    split = Mesh(chips, DATA + MODEL)
    return jax.shard_map(
        shards,
        mesh=split,
        in_specs=(P(DATA, MODEL), P(DATA, MODEL), P(DATA, MODEL), P(DATA), P(), P()),
        out_specs=P(MODEL, DATA),
        check_vma=False,
    )
```

```python
import math

import jax
import jax.numpy as jnp
from jax import lax
from jax.sharding import Mesh, PartitionSpec as P

D = 8192
HEAD_DIM = 128


EPSILON = 1e-06

CHIPS = ("z", "y_hi")
CORE = "core"
DATA = CHIPS + (CORE,)
MODEL = ("x", "y_lo")
PAIR = (CORE,) + MODEL


def attend(queries, key_rows, value_rows):
    length = queries.shape[0]
    kv_heads = key_rows.shape[1] // HEAD_DIM
    group_size = queries.shape[1] // HEAD_DIM // kv_heads
    query_four = queries.reshape(length, kv_heads, group_size, HEAD_DIM)
    key_three = key_rows.reshape(length, kv_heads, HEAD_DIM)
    value_three = value_rows.reshape(length, kv_heads, HEAD_DIM)
    scores = jnp.einsum(
        "tkgd,skd->kgts", query_four, key_three, preferred_element_type=jnp.float32
    ) / math.sqrt(HEAD_DIM)
    row_position = lax.broadcasted_iota(jnp.int32, (length, length), 0)
    column_position = lax.broadcasted_iota(jnp.int32, (length, length), 1)
    scores = jnp.where(column_position <= row_position, scores, -jnp.inf)
    weights = jax.nn.softmax(scores, axis=-1).astype(jnp.bfloat16)
    mixture = jnp.einsum(
        "kgts,skd->tkgd", weights, value_three, preferred_element_type=jnp.float32
    )
    return mixture.astype(jnp.bfloat16).reshape(length, queries.shape[1])


def squares_by_row(matrix):
    return jnp.sum(jnp.square(matrix.astype(jnp.float32)), axis=-1)


def inner_rows(left, right):
    return lax.dot_general(
        left, right, (((1,), (1,)), ((), ())), preferred_element_type=jnp.float32
    )


def attend_rows(queries, key_rows, value_rows, rows, start):
    length = queries.shape[0]
    kv_heads = key_rows.shape[1] // HEAD_DIM
    group_size = queries.shape[1] // HEAD_DIM // kv_heads
    picked = pick_rows(queries, rows, start)
    query_four = picked.reshape(rows.shape[0], kv_heads, group_size, HEAD_DIM)
    key_three = key_rows.reshape(length, kv_heads, HEAD_DIM)
    value_three = value_rows.reshape(length, kv_heads, HEAD_DIM)
    scores = jnp.einsum(
        "tkgd,skd->kgts", query_four, key_three, preferred_element_type=jnp.float32
    ) / math.sqrt(HEAD_DIM)
    column_position = lax.broadcasted_iota(jnp.int32, (rows.shape[0], length), 1)
    scores = jnp.where(column_position + start <= rows[:, None], scores, -jnp.inf)
    weights = jax.nn.softmax(scores, axis=-1).astype(jnp.bfloat16)
    mixture = jnp.einsum(
        "kgts,skd->tkgd", weights, value_three, preferred_element_type=jnp.float32
    )
    return mixture.astype(jnp.bfloat16).reshape(rows.shape[0], queries.shape[1])


def pick_rows(matrix, rows, start):
    hits = rows[:, None] == start + lax.broadcasted_iota(jnp.int32, (rows.shape[0], matrix.shape[0]), 1)
    return jnp.dot(
        hits.astype(matrix.dtype), matrix, preferred_element_type=jnp.float32
    ).astype(matrix.dtype)


def swap_cores(piece):
    return lax.ppermute(piece, CORE, [(0, 1), (1, 0)])


def gather_marks(query_marks, output_marks):
    data_count = lax.axis_size(DATA)
    kinds = jnp.stack([query_marks, output_marks])
    spread = jnp.broadcast_to(kinds[None], (data_count // 2,) + kinds.shape)
    return lax.all_to_all(
        spread.reshape((data_count,) + query_marks.shape), DATA, 0, 0, tiled=True
    )


def broadcast_gather(piece, axis_name):
    count = lax.axis_size(axis_name)
    spread = jnp.broadcast_to(piece[None], (count,) + piece.shape)
    return lax.all_to_all(spread, axis_name, 0, 0, tiled=True)


def shards(queries, key_rows, value_rows, landmark_index, radius_in, radius_out):
    length = queries.shape[0]
    model_count = lax.axis_size(MODEL)
    data_count = lax.axis_size(DATA)
    model_index = lax.axis_index(MODEL)
    landmarks = radius_in.shape[0]
    row_share = landmarks // model_count
    column_share = landmarks // data_count
    token_count = length * data_count

    start = lax.axis_index(DATA) * length
    first = lax.axis_index(CORE) == 0
    marks = gather_marks(
        pick_rows(queries, landmark_index, start),
        attend_rows(queries, key_rows, value_rows, landmark_index, start),
    ).reshape(landmarks, queries.shape[1])
    attended = attend(queries, key_rows, value_rows)
    swapped = swap_cores(jnp.where(first, attended, queries))
    tokens = [jnp.where(first, queries, swapped), jnp.where(first, swapped, attended)]

    mark_norms = squares_by_row(marks)
    distance_part = jnp.stack(
        [
            (
                mark_norms[:, None]
                + squares_by_row(rows)[None, :]
                - 2.0 * inner_rows(marks, rows)
            ).reshape(model_count, row_share, length)
            for rows in tokens
        ]
    ).reshape(2 * model_count, row_share, length)
    received = lax.all_to_all(distance_part, PAIR, 0, 0, tiled=True)
    distance = jnp.sum(received.reshape(2, model_count, row_share, length), axis=1)

    widths = lax.dynamic_slice_in_dim(
        jnp.stack([radius_in, radius_out]), model_index * row_share, row_share, 1
    )
    features = jnp.exp(-distance / (D * widths[:, :, None])).astype(jnp.bfloat16)
    row_features = features[0]
    own_columns = features[1]
    column_features = broadcast_gather(own_columns, MODEL).reshape(landmarks, length)

    rows32 = row_features.astype(jnp.float32)
    columns32 = column_features.astype(jnp.float32)
    row_mean = jnp.mean(rows32, axis=1)
    column_mean = jnp.mean(columns32, axis=1)
    rows_centered = (rows32 - row_mean[:, None]).astype(jnp.bfloat16)
    columns_centered = (columns32 - column_mean[:, None]).astype(jnp.bfloat16)
    second = lax.dot_general(
        rows_centered,
        columns_centered,
        (((1,), (1,)), ((), ())),
        preferred_element_type=jnp.float32,
    )
    row_square = jnp.sum(jnp.square(rows_centered.astype(jnp.float32)), axis=1)
    column_square = jnp.sum(jnp.square(columns_centered.astype(jnp.float32)), axis=1)

    packed = jnp.concatenate(
        [
            jnp.transpose(
                second.reshape(row_share, data_count, column_share), (1, 0, 2)
            ).reshape(data_count, row_share * column_share),
            jnp.broadcast_to(row_mean[None], (data_count, row_share)),
            jnp.broadcast_to(row_square[None], (data_count, row_share)),
            column_mean.reshape(data_count, column_share),
            column_square.reshape(data_count, column_share),
        ],
        axis=1,
    )
    received = lax.all_to_all(packed, DATA, 0, 0, tiled=True)
    cut = row_share * column_share
    second_parts = received[:, :cut].reshape(data_count, row_share, column_share)
    row_means = received[:, cut : cut + row_share]
    row_squares = received[:, cut + row_share : cut + 2 * row_share]
    column_means = received[:, cut + 2 * row_share : cut + 2 * row_share + column_share]
    column_squares = received[:, cut + 2 * row_share + column_share :]

    row_shift = row_means - jnp.mean(row_means, axis=0)[None, :]
    column_shift = column_means - jnp.mean(column_means, axis=0)[None, :]
    between = jnp.sum(row_shift[:, :, None] * column_shift[:, None, :], axis=0)
    covariance = (jnp.sum(second_parts, axis=0) + length * between) / token_count
    spread_rows = (
        jnp.sum(row_squares, axis=0) + length * jnp.sum(jnp.square(row_shift), axis=0)
    ) / token_count
    spread_columns = (
        jnp.sum(column_squares, axis=0)
        + length * jnp.sum(jnp.square(column_shift), axis=0)
    ) / token_count
    return covariance / jnp.sqrt(
        (spread_rows + EPSILON)[:, None] * (spread_columns + EPSILON)[None, :]
    )


def solution(mesh):
    data_count, model_count = mesh.devices.shape
    chips = mesh.devices.reshape(data_count // 8, 4, 2, model_count // 2, 2)
    split = Mesh(chips, DATA + MODEL)
    return jax.shard_map(
        shards,
        mesh=split,
        in_specs=(P(DATA, MODEL), P(DATA, MODEL), P(DATA, MODEL), P(DATA), P(), P()),
        out_specs=P(MODEL, DATA),
        check_vma=False,
    )
```
